256 devices in a mesh: blk: 32 (over x, y, core), row: 8 (over z).
Axes of the slice: x: 4, y: 4, z: 8, core: 2. Of those that a mesh axis runs over, the one named last changes fastest.
Arguments:
- samples: bfloat16 [1024, 8192], P('blk', 'row'), may hold values from -8 to 8, as said below
- blocks: int32 [64, 4], replicated, may hold values from 0 to 31
- factor: float32 [64, 1024], P(None, 'row'), may hold values from -1.2 to 1.2
Outputs:
- cumulants: float32 [64, 1024, 1024], P('blk', 'row')
- factor_out: float32 [64, 1024], P(None, 'row')
The draws below stay inside these ranges and needn't reach their ends.
Inputs may be any that keep to these rules, and one draw needn't show every extreme that they name: `samples`: channel values are drawn with mean zero.
All inputs are finite; a program needn't handle non-finite values.
Results may differ from the reference program's by a relative error of at most 0.0014.
Values may be sent and summed in bfloat16 or wider, within the bound.
No kernel may reach another device: no remote copies, remote signals or barrier semaphores. Data moves between devices by JAX's collectives and lax.ppermute only.
A program may use at most 64 MiB of HBM per device.

```python
import jax
import jax.numpy as jnp
from jax import lax

CHANNELS = 1024
BLOCK = 32
RANK = 64
SAMPLES = 8192
ITERS = 2
CBLOCKS = 32
NBLOCKS = 64


def draw_samples(key, part):
    first_key = jax.random.fold_in(key, 11)
    noise_key, spread_key, source_key, load_key = jax.random.split(first_key, 4)
    spread = jnp.exp(0.05 * jax.random.normal(spread_key, (SAMPLES,), jnp.float32))
    sources = jax.random.laplace(source_key, (4, SAMPLES), jnp.float32) * 0.70710678
    noise_part = jax.random.normal(noise_key, (CHANNELS, SAMPLES), jnp.float32)
    loadings = 0.5 * jax.random.normal(load_key, (CHANNELS, 4), jnp.float32)
    values = noise_part * spread[None, :]
    for source in range(4):
        values = values + loadings[:, source:source + 1] * sources[source][None, :]
    return jnp.clip(values, -8.0, 8.0).astype(jnp.bfloat16)


def draw_factor(key, part):
    factor_key = jax.random.fold_in(key, 23)
    values = 0.33 * jax.random.normal(factor_key, (RANK, CHANNELS), jnp.float32)
    return jnp.clip(values, -1.2, 1.2)


def place_ends(drawn, rng, smallest, high):
    place = [jax.random.randint(jax.random.fold_in(rng, axis), (), 0, length) for axis, length in enumerate(drawn.shape)]
    longest = drawn.shape.index(max(drawn.shape))
    beside = place[:longest] + [(place[longest] + 1) % drawn.shape[longest]] + place[longest + 1:]
    return drawn.at[tuple(place)].set(smallest).at[tuple(beside)].set(high)


def setup_inputs(seed: int = 0) -> dict:
    key_list = jax.random.split(jax.random.key(seed), 4)
    samples = draw_samples(jax.random.fold_in(key_list[3], 71), 0)
    blocks = place_ends(jax.random.randint(key_list[1], (NBLOCKS, 4), 0, CBLOCKS), jax.random.fold_in(key_list[1], 1), 0, CBLOCKS - 1).astype(jnp.int32)
    factor = draw_factor(jax.random.fold_in(key_list[3], 71), 0)
    return {"samples": samples, "blocks": blocks, "factor": factor}


step_size = 0.2

def pair_rows(left, right):
    product = left[:, None, :].astype(jnp.float32) * right[None, :, :].astype(jnp.float32)
    return product.reshape(left.shape[0] * right.shape[0], left.shape[1]).astype(jnp.bfloat16)

def gauss_terms(gram, count, width, row_lo):
    highest = lax.Precision.HIGHEST

    def part(first, second):
        return gram[first * width:(first + 1) * width, second * width:(second + 1) * width]
    cov_ab = lax.dynamic_slice_in_dim(part(0, 1), row_lo, count, 0)
    cov_ac = lax.dynamic_slice_in_dim(part(0, 2), row_lo, count, 0)
    cov_ad = lax.dynamic_slice_in_dim(part(0, 3), row_lo, count, 0)
    cov_cd = part(2, 3)
    cov_bd = part(1, 3)
    cov_bc = part(1, 2)
    first_term = cov_ab.reshape(-1)[:, None] * cov_cd.reshape(-1)[None, :]
    second_term = jnp.einsum('ik,jl->ijkl', cov_ac, cov_bd, precision=highest).reshape(count * width, width * width)
    third_term = jnp.einsum('il,jk->ijkl', cov_ad, cov_bc, precision=highest).reshape(count * width, width * width)
    return first_term + second_term + third_term

def add_cols(total, piece, start):
    old = lax.dynamic_slice_in_dim(total, start, piece.shape[1], 1)
    return lax.dynamic_update_slice_in_dim(total, old + piece, start, 1)

def add_grads(total, kslab, full, ids, row_lo, count, width):
    highest = lax.Precision.HIGHEST
    rank = full.shape[0]
    start_a = ids[0] * width + row_lo
    fac_a = lax.dynamic_slice_in_dim(full, start_a, count, 1)
    fac_b = lax.dynamic_slice_in_dim(full, ids[1] * width, width, 1)
    fac_c = lax.dynamic_slice_in_dim(full, ids[2] * width, width, 1)
    fac_d = lax.dynamic_slice_in_dim(full, ids[3] * width, width, 1)
    upair = (fac_a[:, :, None] * fac_b[:, None, :]).reshape(rank, count * width)
    vpair = (fac_c[:, :, None] * fac_d[:, None, :]).reshape(rank, width * width)
    model = lax.dot_general(upair, vpair, (((0,), (0,)), ((), ())), precision=highest)
    resid = kslab - model
    wmat = lax.dot_general(vpair, resid, (((1,), (1,)), ((), ())), precision=highest).reshape(rank, count, width)
    zmat = jnp.dot(upair, resid, precision=highest).reshape(rank, width, width)
    total = add_cols(total, lax.optimization_barrier(jnp.sum(wmat * fac_b[:, None, :], axis=2)), start_a)
    total = add_cols(total, lax.optimization_barrier(jnp.sum(wmat * fac_a[:, :, None], axis=1)), ids[1] * width)
    total = add_cols(total, lax.optimization_barrier(jnp.sum(zmat * fac_d[:, None, :], axis=2)), ids[2] * width)
    total = add_cols(total, lax.optimization_barrier(jnp.sum(zmat * fac_c[:, :, None], axis=1)), ids[3] * width)
    return total

def one_block(samples, ids):
    width = BLOCK
    parts = [lax.dynamic_slice_in_dim(samples, ids[m] * width, width, 0) for m in range(4)]
    pmat = pair_rows(parts[0], parts[1])
    qmat = pair_rows(parts[2], parts[3])
    moment = lax.dot_general(pmat, qmat, (((1,), (1,)), ((), ())), preferred_element_type=jnp.float32) / SAMPLES
    joined = jnp.concatenate(parts, axis=0)
    gram = lax.dot_general(joined, joined, (((1,), (1,)), ((), ())), preferred_element_type=jnp.float32) / SAMPLES
    return moment - gauss_terms(gram, width, width, 0)

def reference(samples, blocks, factor):
    cumulants = lax.map(lambda ids: one_block(samples, ids), blocks)
    current = factor
    for step in range(ITERS):

        def add_block(total, pair, full=current):
            kslab, ids = pair
            return (add_grads(total, kslab, full, ids, 0, BLOCK, BLOCK), None)
        grad, unused = lax.scan(add_block, jnp.zeros_like(current), (cumulants, blocks))
        scale = lax.rsqrt(jnp.mean(grad * grad) + 1e-06)
        current = current + step_size * scale * grad
    return (cumulants, current)
```

```python
import jax
import jax.numpy as jnp
from jax import lax
from jax.sharding import PartitionSpec as P

CHANNELS = 1024
BLOCK = 32
RANK = 64
SAMPLES = 8192
ITERS = 2


step_size = 0.2


def pair_rows(left, right):
    product = left[:, None, :].astype(jnp.float32) * right[None, :, :].astype(jnp.float32)
    return product.reshape(left.shape[0] * right.shape[0], left.shape[1]).astype(jnp.bfloat16)


def contract_last(left, right):
    return lax.dot_general(
        left, right, (((1,), (1,)), ((), ())), preferred_element_type=jnp.float32
    )


def gauss_terms(gram, count, width, row_lo):
    highest = lax.Precision.HIGHEST

    def part(first, second):
        return gram[first * width : (first + 1) * width, second * width : (second + 1) * width]

    cov_ab = lax.dynamic_slice_in_dim(part(0, 1), row_lo, count, 0)
    cov_ac = lax.dynamic_slice_in_dim(part(0, 2), row_lo, count, 0)
    cov_ad = lax.dynamic_slice_in_dim(part(0, 3), row_lo, count, 0)
    cov_cd = part(2, 3)
    cov_bd = part(1, 3)
    cov_bc = part(1, 2)
    first_term = cov_ab.reshape(-1)[:, None] * cov_cd.reshape(-1)[None, :]
    second_term = jnp.einsum("ik,jl->ijkl", cov_ac, cov_bd, precision=highest).reshape(
        count * width, width * width
    )
    third_term = jnp.einsum("il,jk->ijkl", cov_ad, cov_bc, precision=highest).reshape(
        count * width, width * width
    )
    return first_term + second_term + third_term


def add_cols(total, piece, start):
    old = lax.dynamic_slice_in_dim(total, start, piece.shape[1], 1)
    return lax.dynamic_update_slice_in_dim(total, old + piece, start, 1)


def add_grads(total, kslab, full, ids, row_lo, count, width):
    highest = lax.Precision.HIGHEST
    rank = full.shape[0]
    start_a = ids[0] * width + row_lo
    fac_a = lax.dynamic_slice_in_dim(full, start_a, count, 1)
    fac_b = lax.dynamic_slice_in_dim(full, ids[1] * width, width, 1)
    fac_c = lax.dynamic_slice_in_dim(full, ids[2] * width, width, 1)
    fac_d = lax.dynamic_slice_in_dim(full, ids[3] * width, width, 1)
    upair = (fac_a[:, :, None] * fac_b[:, None, :]).reshape(rank, count * width)
    vpair = (fac_c[:, :, None] * fac_d[:, None, :]).reshape(rank, width * width)
    model = lax.dot_general(upair, vpair, (((0,), (0,)), ((), ())), precision=highest)
    resid = kslab - model
    wmat = lax.dot_general(vpair, resid, (((1,), (1,)), ((), ())), precision=highest).reshape(
        rank, count, width
    )
    zmat = jnp.dot(upair, resid, precision=highest).reshape(rank, width, width)
    total = add_cols(total, jnp.sum(wmat * fac_b[:, None, :], axis=2), start_a)
    total = add_cols(total, jnp.sum(wmat * fac_a[:, :, None], axis=1), ids[1] * width)
    total = add_cols(total, jnp.sum(zmat * fac_d[:, None, :], axis=2), ids[2] * width)
    total = add_cols(total, jnp.sum(zmat * fac_c[:, :, None], axis=1), ids[3] * width)
    return total


def gather_factor(columns):
    return lax.all_gather(columns, "row", axis=1, tiled=True)


def all_sum(value):
    for axis in ("row", "blk"):
        size = lax.axis_size(axis)
        stride = 1
        while stride < size:
            pairs = [(index, index ^ stride) for index in range(size)]
            value = value + lax.ppermute(value, axis, pairs)
            stride *= 2
    return value


def per_device(samples, blocks, factor):
    width = BLOCK
    row_count = lax.axis_size("row")
    count = width // row_count
    row_lo = lax.axis_index("row") * count
    per_owner = blocks.shape[0] // lax.axis_size("blk")
    mine = lax.dynamic_slice_in_dim(blocks, lax.axis_index("blk") * per_owner, per_owner, 0)
    needed = mine.reshape(-1)
    pairs = width * width
    piece = lax.all_gather(samples, "blk", axis=0, tiled=True)
    pieces = piece.shape[0] // width
    owned = jnp.arange(pieces, dtype=jnp.int32)
    select = (needed[:, None] == owned[None, :]).astype(jnp.bfloat16)
    shaped = piece.reshape(pieces, width, piece.shape[1])
    taken = jnp.einsum("mb,bcs->mcs", select, shaped, preferred_element_type=jnp.float32)
    local = taken.astype(jnp.bfloat16)
    slabs = []
    whole = lax.all_gather(local, "row", axis=2, tiled=True)
    sample_block = min(SAMPLES, 2048)
    for slot in range(per_owner):
        source_a = whole[4 * slot]
        source_b = whole[4 * slot + 1]
        source_c = whole[4 * slot + 2]
        source_d = whole[4 * slot + 3]

        def accumulate(index, moment):
            low = index * sample_block
            left = lax.dynamic_slice(source_a, (row_lo, low), (count, sample_block))
            right = lax.dynamic_slice_in_dim(source_b, low, sample_block, 1)
            third = lax.dynamic_slice_in_dim(source_c, low, sample_block, 1)
            fourth = lax.dynamic_slice_in_dim(source_d, low, sample_block, 1)
            pmat = pair_rows(left, right)
            qmat = pair_rows(third, fourth)
            return moment + contract_last(pmat, qmat)

        moment = lax.fori_loop(
            0, SAMPLES // sample_block, accumulate, jnp.zeros((count * width, pairs), jnp.float32)
        )
        moment = moment / SAMPLES
        joined = whole[4 * slot : 4 * slot + 4].reshape(4 * width, whole.shape[2])
        gram = contract_last(joined, joined) / SAMPLES
        slabs.append(moment - gauss_terms(gram, count, width, row_lo))
    full = gather_factor(factor)
    for step in range(ITERS):
        grad = jnp.zeros(full.shape, jnp.float32)
        for slot in range(per_owner):
            grad = add_grads(grad, slabs[slot], full, mine[slot], row_lo, count, width)
        grad = all_sum(grad)
        scale = lax.rsqrt(jnp.mean(grad * grad) + 1e-06)
        full = full + step_size * scale * grad
    col_count = factor.shape[1]
    columns = lax.dynamic_slice_in_dim(full, lax.axis_index("row") * col_count, col_count, 1)
    return (jnp.stack(slabs), columns)


def solution(mesh):
    placed = (P("blk", "row"), P(), P(None, "row"))
    return jax.shard_map(
        per_device,
        mesh=mesh,
        in_specs=placed,
        out_specs=(P("blk", "row", None), P(None, "row")),
        check_vma=False,
    )
```

```python
import jax
import jax.numpy as jnp
from jax import lax
from jax.sharding import PartitionSpec as P

CHANNELS = 1024
BLOCK = 32
RANK = 64
SAMPLES = 8192
ITERS = 2


step_size = 0.2


def pair_rows(left, right):
    product = left[:, None, :].astype(jnp.float32) * right[None, :, :].astype(jnp.float32)
    return product.reshape(left.shape[0] * right.shape[0], left.shape[1]).astype(jnp.bfloat16)


def contract_last(left, right):
    return lax.dot_general(
        left, right, (((1,), (1,)), ((), ())), preferred_element_type=jnp.float32
    )


def gauss_terms(gram, count, width, row_lo):
    highest = lax.Precision.HIGHEST

    def part(first, second):
        return gram[first * width : (first + 1) * width, second * width : (second + 1) * width]

    cov_ab = lax.dynamic_slice_in_dim(part(0, 1), row_lo, count, 0)
    cov_ac = lax.dynamic_slice_in_dim(part(0, 2), row_lo, count, 0)
    cov_ad = lax.dynamic_slice_in_dim(part(0, 3), row_lo, count, 0)
    cov_cd = part(2, 3)
    cov_bd = part(1, 3)
    cov_bc = part(1, 2)
    first_term = cov_ab.reshape(-1)[:, None] * cov_cd.reshape(-1)[None, :]
    second_term = jnp.einsum("ik,jl->ijkl", cov_ac, cov_bd, precision=highest).reshape(
        count * width, width * width
    )
    third_term = jnp.einsum("il,jk->ijkl", cov_ad, cov_bc, precision=highest).reshape(
        count * width, width * width
    )
    return first_term + second_term + third_term


def add_cols(total, piece, start):
    old = lax.dynamic_slice_in_dim(total, start, piece.shape[1], 1)
    return lax.dynamic_update_slice_in_dim(total, old + piece, start, 1)


def add_grads(total, kslab, full, ids, row_lo, count, width):
    highest = lax.Precision.HIGHEST
    rank = full.shape[0]
    start_a = ids[0] * width + row_lo
    fac_a = lax.dynamic_slice_in_dim(full, start_a, count, 1)
    fac_b = lax.dynamic_slice_in_dim(full, ids[1] * width, width, 1)
    fac_c = lax.dynamic_slice_in_dim(full, ids[2] * width, width, 1)
    fac_d = lax.dynamic_slice_in_dim(full, ids[3] * width, width, 1)
    upair = (fac_a[:, :, None] * fac_b[:, None, :]).reshape(rank, count * width)
    vpair = (fac_c[:, :, None] * fac_d[:, None, :]).reshape(rank, width * width)
    model = lax.dot_general(upair, vpair, (((0,), (0,)), ((), ())), precision=highest)
    resid = kslab - model
    wmat = lax.dot_general(vpair, resid, (((1,), (1,)), ((), ())), precision=highest).reshape(
        rank, count, width
    )
    zmat = jnp.dot(upair, resid, precision=highest).reshape(rank, width, width)
    total = add_cols(total, jnp.sum(wmat * fac_b[:, None, :], axis=2), start_a)
    total = add_cols(total, jnp.sum(wmat * fac_a[:, :, None], axis=1), ids[1] * width)
    total = add_cols(total, jnp.sum(zmat * fac_d[:, None, :], axis=2), ids[2] * width)
    total = add_cols(total, jnp.sum(zmat * fac_c[:, :, None], axis=1), ids[3] * width)
    return total


def gather_factor(columns):
    stacked = lax.all_gather(columns, "row", axis=0)
    return jnp.transpose(stacked, (1, 0, 2)).reshape(columns.shape[0], -1)


def swap(value, axis, stride):
    size = lax.axis_size(axis)
    return lax.ppermute(value, axis, [(index, index ^ stride) for index in range(size)])


def all_sum(value):
    shape = value.shape
    value = value.reshape(-1, 128)
    upper = lax.axis_index("blk") % 2
    half = value.shape[0] // 2
    low, high = value[:half], value[half:]
    keep = jnp.where(upper == 0, low, high)
    value = keep + swap(jnp.where(upper == 0, high, low), "blk", 1)
    for axis in ("blk", "row"):
        stride = 2 if axis == "blk" else 1
        while stride < lax.axis_size(axis):
            value = value + swap(value, axis, stride)
            stride *= 2
    other = swap(value, "blk", 1)
    value = jnp.where(upper == 0, jnp.concatenate([value, other]), jnp.concatenate([other, value]))
    return value.reshape(shape)


def per_device(samples, blocks, factor):
    width = BLOCK
    row_count = lax.axis_size("row")
    count = width // row_count
    row_lo = lax.axis_index("row") * count
    per_owner = blocks.shape[0] // lax.axis_size("blk")
    mine = lax.dynamic_slice_in_dim(blocks, lax.axis_index("blk") * per_owner, per_owner, 0)
    needed = mine.reshape(-1)
    pairs = width * width
    piece = lax.all_gather(samples, "blk", axis=0, tiled=True)
    pieces = piece.shape[0] // width
    owned = jnp.arange(pieces, dtype=jnp.int32)
    select = (needed[:, None] == owned[None, :]).astype(jnp.bfloat16)
    shaped = piece.reshape(pieces, width, piece.shape[1])
    taken = jnp.einsum("mb,bcs->mcs", select, shaped, preferred_element_type=jnp.float32)
    local = taken.astype(jnp.bfloat16)
    slabs = []
    whole = lax.all_gather(local, "row", axis=2, tiled=True)
    sample_block = min(SAMPLES, 2048)
    for slot in range(per_owner):
        source_a = whole[4 * slot]
        source_b = whole[4 * slot + 1]
        source_c = whole[4 * slot + 2]
        source_d = whole[4 * slot + 3]

        def accumulate(index, moment):
            low = index * sample_block
            left = lax.dynamic_slice(source_a, (row_lo, low), (count, sample_block))
            right = lax.dynamic_slice_in_dim(source_b, low, sample_block, 1)
            third = lax.dynamic_slice_in_dim(source_c, low, sample_block, 1)
            fourth = lax.dynamic_slice_in_dim(source_d, low, sample_block, 1)
            pmat = pair_rows(left, right)
            qmat = pair_rows(third, fourth)
            return moment + contract_last(pmat, qmat)

        moment = lax.fori_loop(
            0, SAMPLES // sample_block, accumulate, jnp.zeros((count * width, pairs), jnp.float32)
        )
        moment = moment / SAMPLES
        joined = whole[4 * slot : 4 * slot + 4].reshape(4 * width, whole.shape[2])
        gram = contract_last(joined, joined) / SAMPLES
        slabs.append(moment - gauss_terms(gram, count, width, row_lo))
    full = gather_factor(factor)
    for step in range(ITERS):
        grad = jnp.zeros(full.shape, jnp.float32)
        for slot in range(per_owner):
            grad = add_grads(grad, slabs[slot], full, mine[slot], row_lo, count, width)
        grad = all_sum(grad)
        scale = lax.rsqrt(jnp.mean(grad * grad) + 1e-06)
        full = full + step_size * scale * grad
    col_count = factor.shape[1]
    columns = lax.dynamic_slice_in_dim(full, lax.axis_index("row") * col_count, col_count, 1)
    return (jnp.stack(slabs), columns)


def solution(mesh):
    placed = (P("blk", "row"), P(), P(None, "row"))
    return jax.shard_map(
        per_device,
        mesh=mesh,
        in_specs=placed,
        out_specs=(P("blk", "row", None), P(None, "row")),
        check_vma=False,
    )
```

```python
import jax
import jax.numpy as jnp
from jax import lax
from jax.sharding import PartitionSpec as P

CHANNELS = 1024
BLOCK = 32
RANK = 64
SAMPLES = 8192
ITERS = 2


step_size = 0.2


def pair_rows(left, right):
    product = left[:, None, :].astype(jnp.float32) * right[None, :, :].astype(jnp.float32)
    return product.reshape(left.shape[0] * right.shape[0], left.shape[1]).astype(jnp.bfloat16)


def contract_last(left, right):
    return lax.dot_general(
        left, right, (((1,), (1,)), ((), ())), preferred_element_type=jnp.float32
    )


def gauss_terms(gram, count, width, row_lo):
    highest = lax.Precision.HIGHEST

    def part(first, second):
        return gram[first * width : (first + 1) * width, second * width : (second + 1) * width]

    cov_ab = lax.dynamic_slice_in_dim(part(0, 1), row_lo, count, 0)
    cov_ac = lax.dynamic_slice_in_dim(part(0, 2), row_lo, count, 0)
    cov_ad = lax.dynamic_slice_in_dim(part(0, 3), row_lo, count, 0)
    cov_cd = part(2, 3)
    cov_bd = part(1, 3)
    cov_bc = part(1, 2)
    first_term = cov_ab.reshape(-1)[:, None] * cov_cd.reshape(-1)[None, :]
    second_term = jnp.einsum("ik,jl->ijkl", cov_ac, cov_bd, precision=highest).reshape(
        count * width, width * width
    )
    third_term = jnp.einsum("il,jk->ijkl", cov_ad, cov_bc, precision=highest).reshape(
        count * width, width * width
    )
    return first_term + second_term + third_term


def add_cols(total, piece, start):
    old = lax.dynamic_slice_in_dim(total, start, piece.shape[1], 1)
    return lax.dynamic_update_slice_in_dim(total, old + piece, start, 1)


def add_grads(total, kslab, full, ids, row_lo, count, width):
    highest = lax.Precision.HIGHEST
    rank = full.shape[0]
    start_a = ids[0] * width + row_lo
    fac_a = lax.dynamic_slice_in_dim(full, start_a, count, 1)
    fac_b = lax.dynamic_slice_in_dim(full, ids[1] * width, width, 1)
    fac_c = lax.dynamic_slice_in_dim(full, ids[2] * width, width, 1)
    fac_d = lax.dynamic_slice_in_dim(full, ids[3] * width, width, 1)
    upair = (fac_a[:, :, None] * fac_b[:, None, :]).reshape(rank, count * width)
    vpair = (fac_c[:, :, None] * fac_d[:, None, :]).reshape(rank, width * width)
    model = lax.dot_general(upair, vpair, (((0,), (0,)), ((), ())), precision=highest)
    resid = kslab - model
    wmat = lax.dot_general(vpair, resid, (((1,), (1,)), ((), ())), precision=highest).reshape(
        rank, count, width
    )
    zmat = jnp.dot(upair, resid, precision=highest).reshape(rank, width, width)
    total = add_cols(total, jnp.sum(wmat * fac_b[:, None, :], axis=2), start_a)
    total = add_cols(total, jnp.sum(wmat * fac_a[:, :, None], axis=1), ids[1] * width)
    total = add_cols(total, jnp.sum(zmat * fac_d[:, None, :], axis=2), ids[2] * width)
    total = add_cols(total, jnp.sum(zmat * fac_c[:, :, None], axis=1), ids[3] * width)
    return total


def gather_factor(columns):
    stacked = lax.all_gather(columns, "row", axis=0)
    return jnp.transpose(stacked, (1, 0, 2)).reshape(columns.shape[0], -1)


def swap(value, axis, stride):
    size = lax.axis_size(axis)
    return lax.ppermute(value, axis, [(index, index ^ stride) for index in range(size)])


def all_sum(value):
    shape = value.shape
    value = value.reshape(-1, 128)
    upper = lax.axis_index("blk") % 2
    half = value.shape[0] // 2
    low, high = value[:half], value[half:]
    keep = jnp.where(upper == 0, low, high)
    value = keep + swap(jnp.where(upper == 0, high, low), "blk", 1)
    for axis in ("blk", "row"):
        stride = 2 if axis == "blk" else 1
        while stride < lax.axis_size(axis):
            value = value + swap(value, axis, stride)
            stride *= 2
    other = swap(value, "blk", 1)
    value = jnp.where(upper == 0, jnp.concatenate([value, other]), jnp.concatenate([other, value]))
    return value.reshape(shape)


def per_device(samples, blocks, factor):
    width = BLOCK
    row_count = lax.axis_size("row")
    count = width // row_count
    row_lo = lax.axis_index("row") * count
    per_owner = blocks.shape[0] // lax.axis_size("blk")
    mine = lax.dynamic_slice_in_dim(blocks, lax.axis_index("blk") * per_owner, per_owner, 0)
    needed = mine.reshape(-1)
    pairs = width * width
    piece = lax.all_gather(samples, "blk", axis=0, tiled=True)
    pieces = piece.shape[0] // width
    owned = jnp.arange(pieces, dtype=jnp.int32)
    select = (needed[:, None] == owned[None, :]).astype(jnp.bfloat16)
    shaped = piece.reshape(pieces, width, piece.shape[1])
    taken = jnp.einsum("mb,bcs->mcs", select, shaped, preferred_element_type=jnp.float32)
    chunk = taken.astype(jnp.bfloat16)
    ring = [(index, (index + 1) % row_count) for index in range(row_count)]
    piece_rows = 4 * width
    moments = [jnp.zeros((count * width, pairs), jnp.float32) for _ in range(per_owner)]
    grams = [jnp.zeros((piece_rows, piece_rows), jnp.float32) for _ in range(per_owner)]
    held = factor
    held_pieces = []
    for step in range(row_count):
        if step + 1 < row_count:
            incoming = lax.ppermute(chunk, "row", ring)
            held_in = lax.ppermute(held, "row", ring)
        held_pieces.append(held)
        for slot in range(per_owner):
            left = lax.dynamic_slice_in_dim(chunk[4 * slot], row_lo, count, 0)
            pmat = pair_rows(left, chunk[4 * slot + 1])
            qmat = pair_rows(chunk[4 * slot + 2], chunk[4 * slot + 3])
            moments[slot] = moments[slot] + contract_last(pmat, qmat)
            joined = chunk[4 * slot : 4 * slot + 4].reshape(piece_rows, chunk.shape[2])
            grams[slot] = grams[slot] + contract_last(joined, joined)
        if step + 1 < row_count:
            chunk, held = incoming, held_in
    slabs = []
    for slot in range(per_owner):
        moment = moments[slot] / SAMPLES
        gram = grams[slot] / SAMPLES
        slabs.append(moment - gauss_terms(gram, count, width, row_lo))
    source = (lax.axis_index("row") - jnp.arange(row_count)) % row_count
    stacked = jnp.stack(held_pieces)[source]
    full = jnp.transpose(stacked, (1, 0, 2)).reshape(factor.shape[0], -1)
    for step in range(ITERS):
        grad = jnp.zeros(full.shape, jnp.float32)
        for slot in range(per_owner):
            grad = add_grads(grad, slabs[slot], full, mine[slot], row_lo, count, width)
        grad = all_sum(grad)
        scale = lax.rsqrt(jnp.mean(grad * grad) + 1e-06)
        full = full + step_size * scale * grad
    col_count = factor.shape[1]
    columns = lax.dynamic_slice_in_dim(full, lax.axis_index("row") * col_count, col_count, 1)
    return (jnp.stack(slabs), columns)


def solution(mesh):
    placed = (P("blk", "row"), P(), P(None, "row"))
    return jax.shard_map(
        per_device,
        mesh=mesh,
        in_specs=placed,
        out_specs=(P("blk", "row", None), P(None, "row")),
        check_vma=False,
    )
```

```python
import jax
import jax.numpy as jnp
from jax import lax
from jax.sharding import PartitionSpec as P

CHANNELS = 1024
BLOCK = 32
RANK = 64
SAMPLES = 8192
ITERS = 2


step_size = 0.2


def pair_rows(left, right):
    product = left[:, None, :].astype(jnp.float32) * right[None, :, :].astype(jnp.float32)
    return product.reshape(left.shape[0] * right.shape[0], left.shape[1]).astype(jnp.bfloat16)


def contract_last(left, right):
    return lax.dot_general(
        left, right, (((1,), (1,)), ((), ())), preferred_element_type=jnp.float32
    )


def gauss_terms(gram, count, width, row_lo):
    highest = lax.Precision.HIGHEST

    def part(first, second):
        return gram[first * width : (first + 1) * width, second * width : (second + 1) * width]

    cov_ab = lax.dynamic_slice_in_dim(part(0, 1), row_lo, count, 0)
    cov_ac = lax.dynamic_slice_in_dim(part(0, 2), row_lo, count, 0)
    cov_ad = lax.dynamic_slice_in_dim(part(0, 3), row_lo, count, 0)
    cov_cd = part(2, 3)
    cov_bd = part(1, 3)
    cov_bc = part(1, 2)
    first_term = cov_ab.reshape(-1)[:, None] * cov_cd.reshape(-1)[None, :]
    second_term = jnp.einsum("ik,jl->ijkl", cov_ac, cov_bd, precision=highest).reshape(
        count * width, width * width
    )
    third_term = jnp.einsum("il,jk->ijkl", cov_ad, cov_bc, precision=highest).reshape(
        count * width, width * width
    )
    return first_term + second_term + third_term


def add_cols(total, piece, start):
    old = lax.dynamic_slice_in_dim(total, start, piece.shape[1], 1)
    return lax.dynamic_update_slice_in_dim(total, old + piece, start, 1)


def add_grads(total, kslab, full, ids, row_lo, count, width):
    highest = lax.Precision.HIGHEST
    rank = full.shape[0]
    start_a = ids[0] * width + row_lo
    fac_a = lax.dynamic_slice_in_dim(full, start_a, count, 1)
    fac_b = lax.dynamic_slice_in_dim(full, ids[1] * width, width, 1)
    fac_c = lax.dynamic_slice_in_dim(full, ids[2] * width, width, 1)
    fac_d = lax.dynamic_slice_in_dim(full, ids[3] * width, width, 1)
    upair = (fac_a[:, :, None] * fac_b[:, None, :]).reshape(rank, count * width)
    vpair = (fac_c[:, :, None] * fac_d[:, None, :]).reshape(rank, width * width)
    model = lax.dot_general(upair, vpair, (((0,), (0,)), ((), ())), precision=highest)
    resid = kslab - model
    wmat = lax.dot_general(vpair, resid, (((1,), (1,)), ((), ())), precision=highest).reshape(
        rank, count, width
    )
    zmat = jnp.dot(upair, resid, precision=highest).reshape(rank, width, width)
    total = add_cols(total, jnp.sum(wmat * fac_b[:, None, :], axis=2), start_a)
    total = add_cols(total, jnp.sum(wmat * fac_a[:, :, None], axis=1), ids[1] * width)
    total = add_cols(total, jnp.sum(zmat * fac_d[:, None, :], axis=2), ids[2] * width)
    total = add_cols(total, jnp.sum(zmat * fac_c[:, :, None], axis=1), ids[3] * width)
    return total


def gather_factor(columns):
    stacked = lax.all_gather(columns, "row", axis=0)
    return jnp.transpose(stacked, (1, 0, 2)).reshape(columns.shape[0], -1)


def swap(value, axis, stride):
    size = lax.axis_size(axis)
    return lax.ppermute(value, axis, [(index, index ^ stride) for index in range(size)])


def all_sum(value):
    shape = value.shape
    value = value.reshape(-1, 128)
    upper = lax.axis_index("blk") % 2
    half = value.shape[0] // 2
    low, high = value[:half], value[half:]
    keep = jnp.where(upper == 0, low, high)
    value = keep + swap(jnp.where(upper == 0, high, low), "blk", 1)
    for axis in ("blk", "row"):
        stride = 2 if axis == "blk" else 1
        while stride < lax.axis_size(axis):
            value = value + swap(value, axis, stride)
            stride *= 2
    other = swap(value, "blk", 1)
    value = jnp.where(upper == 0, jnp.concatenate([value, other]), jnp.concatenate([other, value]))
    return value.reshape(shape)


def per_device(samples, blocks, factor):
    width = BLOCK
    row_count = lax.axis_size("row")
    count = width // row_count
    row_lo = lax.axis_index("row") * count
    per_owner = blocks.shape[0] // lax.axis_size("blk")
    mine = lax.dynamic_slice_in_dim(blocks, lax.axis_index("blk") * per_owner, per_owner, 0)
    needed = mine.reshape(-1)
    pairs = width * width
    piece = lax.all_gather(samples, "blk", axis=0, tiled=True)
    pieces = piece.shape[0] // width
    owned = jnp.arange(pieces, dtype=jnp.int32)
    select = (needed[:, None] == owned[None, :]).astype(jnp.bfloat16)
    shaped = piece.reshape(pieces, width, piece.shape[1])
    taken = jnp.einsum("mb,bcs->mcs", select, shaped, preferred_element_type=jnp.float32)
    local = taken.astype(jnp.bfloat16)
    forward = [(index, (index + 1) % row_count) for index in range(row_count)]
    backward = [(index, (index - 1) % row_count) for index in range(row_count)]
    piece_rows = 4 * width
    chunks = [local[4 * slot : 4 * slot + 4] for slot in range(per_owner)]
    moments = [jnp.zeros((count * width, pairs), jnp.float32) for _ in range(per_owner)]
    grams = [jnp.zeros((piece_rows, piece_rows), jnp.float32) for _ in range(per_owner)]
    held = factor
    held_pieces = []
    for step in range(row_count):
        if step + 1 < row_count:
            incoming = [
                lax.ppermute(chunks[slot], "row", forward if slot % 2 == 0 else backward)
                for slot in range(per_owner)
            ]
            held_in = lax.ppermute(held, "row", forward)
        held_pieces.append(held)
        for slot in range(per_owner):
            chunk = chunks[slot]
            left = lax.dynamic_slice_in_dim(chunk[0], row_lo, count, 0)
            pmat = pair_rows(left, chunk[1])
            qmat = pair_rows(chunk[2], chunk[3])
            moments[slot] = moments[slot] + contract_last(pmat, qmat)
            joined = chunk.reshape(piece_rows, chunk.shape[2])
            grams[slot] = grams[slot] + contract_last(joined, joined)
        if step + 1 < row_count:
            chunks, held = incoming, held_in
    slabs = []
    for slot in range(per_owner):
        moment = moments[slot] / SAMPLES
        gram = grams[slot] / SAMPLES
        slabs.append(moment - gauss_terms(gram, count, width, row_lo))
    source = (lax.axis_index("row") - jnp.arange(row_count)) % row_count
    stacked = jnp.stack(held_pieces)[source]
    full = jnp.transpose(stacked, (1, 0, 2)).reshape(factor.shape[0], -1)
    for step in range(ITERS):
        grad = jnp.zeros(full.shape, jnp.float32)
        for slot in range(per_owner):
            grad = add_grads(grad, slabs[slot], full, mine[slot], row_lo, count, width)
        grad = all_sum(grad)
        scale = lax.rsqrt(jnp.mean(grad * grad) + 1e-06)
        full = full + step_size * scale * grad
    col_count = factor.shape[1]
    columns = lax.dynamic_slice_in_dim(full, lax.axis_index("row") * col_count, col_count, 1)
    return (jnp.stack(slabs), columns)


def solution(mesh):
    placed = (P("blk", "row"), P(), P(None, "row"))
    return jax.shard_map(
        per_device,
        mesh=mesh,
        in_specs=placed,
        out_specs=(P("blk", "row", None), P(None, "row")),
        check_vma=False,
    )
```

```python
import jax
import jax.numpy as jnp
from jax import lax
from jax.sharding import PartitionSpec as P

CHANNELS = 1024
BLOCK = 32
RANK = 64
SAMPLES = 8192
ITERS = 2


step_size = 0.2


def pair_rows(left, right):
    product = left[:, None, :].astype(jnp.float32) * right[None, :, :].astype(jnp.float32)
    return product.reshape(left.shape[0] * right.shape[0], left.shape[1]).astype(jnp.bfloat16)


def contract_last(left, right):
    return lax.dot_general(
        left, right, (((1,), (1,)), ((), ())), preferred_element_type=jnp.float32
    )


def spread(values, width, major):
    place = jnp.arange(width * width, dtype=jnp.int32)
    index = place // width if major else place % width
    pick = (index[None, :] == jnp.arange(width, dtype=jnp.int32)[:, None]).astype(values.dtype)
    return jnp.dot(values, pick, precision=lax.Precision.HIGHEST)


def cumulant_slab(moment, gram, count, width, row_lo):
    def part(first, second):
        return gram[first * width : (first + 1) * width, second * width : (second + 1) * width]

    cov_ab = lax.dynamic_slice_in_dim(part(0, 1), row_lo, count, 0)
    cov_ac = lax.dynamic_slice_in_dim(part(0, 2), row_lo, count, 0)
    cov_ad = lax.dynamic_slice_in_dim(part(0, 3), row_lo, count, 0)
    cov_cd = part(2, 3)
    cov_bd = part(1, 3)
    cov_bc = part(1, 2)
    first_term = cov_ab[:, :, None] * cov_cd.reshape(1, 1, width * width)
    second_term = spread(cov_ac, width, True)[:, None, :] * spread(cov_bd, width, False)[None, :, :]
    third_term = spread(cov_ad, width, False)[:, None, :] * spread(cov_bc, width, True)[None, :, :]
    shaped = moment.reshape(count, width, width * width)
    slab = shaped - ((first_term + second_term) + third_term)
    return slab.reshape(count * width, width * width)


def add_cols(total, piece, start):
    old = lax.dynamic_slice_in_dim(total, start, piece.shape[1], 1)
    return lax.dynamic_update_slice_in_dim(total, old + piece, start, 1)


def add_grads(total, kslab, full, ids, row_lo, count, width):
    highest = lax.Precision.HIGHEST
    rank = full.shape[0]
    start_a = ids[0] * width + row_lo
    fac_a = lax.dynamic_slice_in_dim(full, start_a, count, 1)
    fac_b = lax.dynamic_slice_in_dim(full, ids[1] * width, width, 1)
    fac_c = lax.dynamic_slice_in_dim(full, ids[2] * width, width, 1)
    fac_d = lax.dynamic_slice_in_dim(full, ids[3] * width, width, 1)
    upair = (fac_a[:, :, None] * fac_b[:, None, :]).reshape(rank, count * width)
    vpair = (fac_c[:, :, None] * fac_d[:, None, :]).reshape(rank, width * width)
    model = lax.dot_general(upair, vpair, (((0,), (0,)), ((), ())), precision=highest)
    resid = kslab - model
    wmat = lax.dot_general(vpair, resid, (((1,), (1,)), ((), ())), precision=highest).reshape(
        rank, count, width
    )
    zmat = jnp.dot(upair, resid, precision=highest).reshape(rank, width, width)
    total = add_cols(total, jnp.sum(wmat * fac_b[:, None, :], axis=2), start_a)
    total = add_cols(total, jnp.sum(wmat * fac_a[:, :, None], axis=1), ids[1] * width)
    total = add_cols(total, jnp.sum(zmat * fac_d[:, None, :], axis=2), ids[2] * width)
    total = add_cols(total, jnp.sum(zmat * fac_c[:, :, None], axis=1), ids[3] * width)
    return total


def gather_factor(columns):
    stacked = lax.all_gather(columns, "row", axis=0)
    return jnp.transpose(stacked, (1, 0, 2)).reshape(columns.shape[0], -1)


def swap(value, axis, stride):
    size = lax.axis_size(axis)
    return lax.ppermute(value, axis, [(index, index ^ stride) for index in range(size)])


def all_sum(value):
    shape = value.shape
    value = value.reshape(-1, 128)
    upper = lax.axis_index("blk") % 2
    half = value.shape[0] // 2
    low, high = value[:half], value[half:]
    keep = jnp.where(upper == 0, low, high)
    value = keep + swap(jnp.where(upper == 0, high, low), "blk", 1)
    for axis in ("blk", "row"):
        stride = 2 if axis == "blk" else 1
        while stride < lax.axis_size(axis):
            value = value + swap(value, axis, stride)
            stride *= 2
    other = swap(value, "blk", 1)
    value = jnp.where(upper == 0, jnp.concatenate([value, other]), jnp.concatenate([other, value]))
    return value.reshape(shape)


def per_device(samples, blocks, factor):
    width = BLOCK
    row_count = lax.axis_size("row")
    count = width // row_count
    row_lo = lax.axis_index("row") * count
    per_owner = blocks.shape[0] // lax.axis_size("blk")
    mine = lax.dynamic_slice_in_dim(blocks, lax.axis_index("blk") * per_owner, per_owner, 0)
    needed = mine.reshape(-1)
    pairs = width * width
    piece = lax.all_gather(samples, "blk", axis=0, tiled=True)
    pieces = piece.shape[0] // width
    owned = jnp.arange(pieces, dtype=jnp.int32)
    select = (needed[:, None] == owned[None, :]).astype(jnp.bfloat16)
    shaped = piece.reshape(pieces, width, piece.shape[1])
    taken = jnp.einsum("mb,bcs->mcs", select, shaped, preferred_element_type=jnp.float32)
    local = taken.astype(jnp.bfloat16)
    forward = [(index, (index + 1) % row_count) for index in range(row_count)]
    backward = [(index, (index - 1) % row_count) for index in range(row_count)]
    piece_rows = 4 * width
    chunks = [local[4 * slot : 4 * slot + 4] for slot in range(per_owner)]
    moments = [jnp.zeros((count * width, pairs), jnp.float32) for _ in range(per_owner)]
    grams = [jnp.zeros((piece_rows, piece_rows), jnp.float32) for _ in range(per_owner)]
    held = factor
    held_pieces = []
    for step in range(row_count):
        if step + 1 < row_count:
            incoming = [
                lax.ppermute(chunks[slot], "row", forward if slot % 2 == 0 else backward)
                for slot in range(per_owner)
            ]
            held_in = lax.ppermute(held, "row", forward)
        held_pieces.append(held)
        for slot in range(per_owner):
            chunk = chunks[slot]
            left = lax.dynamic_slice_in_dim(chunk[0], row_lo, count, 0)
            pmat = pair_rows(left, chunk[1])
            qmat = pair_rows(chunk[2], chunk[3])
            moments[slot] = moments[slot] + contract_last(pmat, qmat)
            joined = chunk.reshape(piece_rows, chunk.shape[2])
            grams[slot] = grams[slot] + contract_last(joined, joined)
        if step + 1 < row_count:
            chunks, held = incoming, held_in
    slabs = []
    for slot in range(per_owner):
        moment = moments[slot] / SAMPLES
        gram = grams[slot] / SAMPLES
        slabs.append(cumulant_slab(moment, gram, count, width, row_lo))
    source = (lax.axis_index("row") - jnp.arange(row_count)) % row_count
    stacked = jnp.stack(held_pieces)[source]
    full = jnp.transpose(stacked, (1, 0, 2)).reshape(factor.shape[0], -1)
    for step in range(ITERS):
        grad = jnp.zeros(full.shape, jnp.float32)
        for slot in range(per_owner):
            grad = add_grads(grad, slabs[slot], full, mine[slot], row_lo, count, width)
        grad = all_sum(grad)
        scale = lax.rsqrt(jnp.mean(grad * grad) + 1e-06)
        full = full + step_size * scale * grad
    col_count = factor.shape[1]
    columns = lax.dynamic_slice_in_dim(full, lax.axis_index("row") * col_count, col_count, 1)
    return (jnp.stack(slabs), columns)


def solution(mesh):
    placed = (P("blk", "row"), P(), P(None, "row"))
    return jax.shard_map(
        per_device,
        mesh=mesh,
        in_specs=placed,
        out_specs=(P("blk", "row", None), P(None, "row")),
        check_vma=False,
    )
```

```python
import jax
import jax.numpy as jnp
from jax import lax
from jax.sharding import PartitionSpec as P

CHANNELS = 1024
BLOCK = 32
RANK = 64
SAMPLES = 8192
ITERS = 2


step_size = 0.2


def pair_rows(left, right):
    product = left[:, None, :].astype(jnp.float32) * right[None, :, :].astype(jnp.float32)
    return product.reshape(left.shape[0] * right.shape[0], left.shape[1]).astype(jnp.bfloat16)


def contract_last(left, right):
    return lax.dot_general(
        left, right, (((1,), (1,)), ((), ())), preferred_element_type=jnp.float32
    )


def spread(values, width, major):
    place = jnp.arange(width * width, dtype=jnp.int32)
    index = place // width if major else place % width
    pick = (index[None, :] == jnp.arange(width, dtype=jnp.int32)[:, None]).astype(values.dtype)
    return jnp.dot(values, pick, precision=lax.Precision.HIGHEST)


def cumulant_slab(moment, gram, count, width, row_lo):
    def part(first, second):
        return gram[first * width : (first + 1) * width, second * width : (second + 1) * width]

    cov_ab = lax.dynamic_slice_in_dim(part(0, 1), row_lo, count, 0)
    cov_ac = lax.dynamic_slice_in_dim(part(0, 2), row_lo, count, 0)
    cov_ad = lax.dynamic_slice_in_dim(part(0, 3), row_lo, count, 0)
    cov_cd = part(2, 3)
    cov_bd = part(1, 3)
    cov_bc = part(1, 2)
    first_term = cov_ab[:, :, None] * cov_cd.reshape(1, 1, width * width)
    second_term = spread(cov_ac, width, True)[:, None, :] * spread(cov_bd, width, False)[None, :, :]
    third_term = spread(cov_ad, width, False)[:, None, :] * spread(cov_bc, width, True)[None, :, :]
    shaped = moment.reshape(count, width, width * width)
    slab = shaped - ((first_term + second_term) + third_term)
    return slab.reshape(count * width, width * width)


def add_cols(total, piece, start):
    old = lax.dynamic_slice_in_dim(total, start, piece.shape[1], 1)
    return lax.dynamic_update_slice_in_dim(total, old + piece, start, 1)


def add_grads(total, kslab, full, ids, row_lo, count, width):
    highest = lax.Precision.HIGHEST
    rank = full.shape[0]
    start_a = ids[0] * width + row_lo
    fac_a = lax.dynamic_slice_in_dim(full, start_a, count, 1)
    fac_b = lax.dynamic_slice_in_dim(full, ids[1] * width, width, 1)
    fac_c = lax.dynamic_slice_in_dim(full, ids[2] * width, width, 1)
    fac_d = lax.dynamic_slice_in_dim(full, ids[3] * width, width, 1)
    upair = (fac_a[:, :, None] * fac_b[:, None, :]).reshape(rank, count * width)
    vpair = (fac_c[:, :, None] * fac_d[:, None, :]).reshape(rank, width * width)
    model = lax.dot_general(upair, vpair, (((0,), (0,)), ((), ())), precision=highest)
    resid = kslab - model
    wmat = lax.dot_general(vpair, resid, (((1,), (1,)), ((), ())), precision=highest).reshape(
        rank, count, width
    )
    zmat = jnp.dot(upair, resid, precision=highest).reshape(rank, width, width)
    total = add_cols(total, jnp.sum(wmat * fac_b[:, None, :], axis=2), start_a)
    total = add_cols(total, jnp.sum(wmat * fac_a[:, :, None], axis=1), ids[1] * width)
    total = add_cols(total, jnp.sum(zmat * fac_d[:, None, :], axis=2), ids[2] * width)
    total = add_cols(total, jnp.sum(zmat * fac_c[:, :, None], axis=1), ids[3] * width)
    return total


def gather_factor(columns):
    stacked = lax.all_gather(columns, "row", axis=0)
    return jnp.transpose(stacked, (1, 0, 2)).reshape(columns.shape[0], -1)


def swap(value, axis, stride):
    size = lax.axis_size(axis)
    return lax.ppermute(value, axis, [(index, index ^ stride) for index in range(size)])


def all_sum(value):
    shape = value.shape
    value = value.reshape(-1, 128)
    upper = lax.axis_index("blk") % 2
    half = value.shape[0] // 2
    low, high = value[:half], value[half:]
    keep = jnp.where(upper == 0, low, high)
    value = keep + swap(jnp.where(upper == 0, high, low), "blk", 1)
    for axis in ("blk", "row"):
        stride = 2 if axis == "blk" else 1
        while stride < lax.axis_size(axis):
            value = value + swap(value, axis, stride)
            stride *= 2
    other = swap(value, "blk", 1)
    value = jnp.where(upper == 0, jnp.concatenate([value, other]), jnp.concatenate([other, value]))
    return value.reshape(shape)


def per_device(samples, blocks, factor):
    width = BLOCK
    row_count = lax.axis_size("row")
    count = width // row_count
    row_lo = lax.axis_index("row") * count
    per_owner = blocks.shape[0] // lax.axis_size("blk")
    mine = lax.dynamic_slice_in_dim(blocks, lax.axis_index("blk") * per_owner, per_owner, 0)
    needed = mine.reshape(-1)
    pairs = width * width
    piece = samples
    stride = 1
    while stride < lax.axis_size("blk"):
        piece = jnp.concatenate([piece, swap(piece, "blk", stride)], axis=0)
        stride *= 2
    pieces = piece.shape[0] // width
    owned = jnp.bitwise_xor(lax.axis_index("blk"), jnp.arange(pieces, dtype=jnp.int32))
    select = (needed[:, None] == owned[None, :]).astype(jnp.bfloat16)
    shaped = piece.reshape(pieces, width, piece.shape[1])
    taken = jnp.einsum("mb,bcs->mcs", select, shaped, preferred_element_type=jnp.float32)
    local = taken.astype(jnp.bfloat16)
    forward = [(index, (index + 1) % row_count) for index in range(row_count)]
    backward = [(index, (index - 1) % row_count) for index in range(row_count)]
    piece_rows = 4 * width
    chunks = [local[4 * slot : 4 * slot + 4] for slot in range(per_owner)]
    moments = [jnp.zeros((count * width, pairs), jnp.float32) for _ in range(per_owner)]
    grams = [jnp.zeros((piece_rows, piece_rows), jnp.float32) for _ in range(per_owner)]
    held = factor
    held_pieces = []
    for step in range(row_count):
        if step + 1 < row_count:
            incoming = [
                lax.ppermute(chunks[slot], "row", forward if slot % 2 == 0 else backward)
                for slot in range(per_owner)
            ]
            held_in = lax.ppermute(held, "row", forward)
        held_pieces.append(held)
        for slot in range(per_owner):
            chunk = chunks[slot]
            left = lax.dynamic_slice_in_dim(chunk[0], row_lo, count, 0)
            pmat = pair_rows(left, chunk[1])
            qmat = pair_rows(chunk[2], chunk[3])
            moments[slot] = moments[slot] + contract_last(pmat, qmat)
            joined = chunk.reshape(piece_rows, chunk.shape[2])
            grams[slot] = grams[slot] + contract_last(joined, joined)
        if step + 1 < row_count:
            chunks, held = incoming, held_in
    slabs = []
    for slot in range(per_owner):
        moment = moments[slot] / SAMPLES
        gram = grams[slot] / SAMPLES
        slabs.append(cumulant_slab(moment, gram, count, width, row_lo))
    source = (lax.axis_index("row") - jnp.arange(row_count)) % row_count
    stacked = jnp.stack(held_pieces)[source]
    full = jnp.transpose(stacked, (1, 0, 2)).reshape(factor.shape[0], -1)
    for step in range(ITERS):
        grad = jnp.zeros(full.shape, jnp.float32)
        for slot in range(per_owner):
            grad = add_grads(grad, slabs[slot], full, mine[slot], row_lo, count, width)
        grad = all_sum(grad)
        scale = lax.rsqrt(jnp.mean(grad * grad) + 1e-06)
        full = full + step_size * scale * grad
    col_count = factor.shape[1]
    columns = lax.dynamic_slice_in_dim(full, lax.axis_index("row") * col_count, col_count, 1)
    return (jnp.stack(slabs), columns)


def solution(mesh):
    placed = (P("blk", "row"), P(), P(None, "row"))
    return jax.shard_map(
        per_device,
        mesh=mesh,
        in_specs=placed,
        out_specs=(P("blk", "row", None), P(None, "row")),
        check_vma=False,
    )
```

```python
import jax
import jax.numpy as jnp
from jax import lax
from jax.sharding import PartitionSpec as P

CHANNELS = 1024
BLOCK = 32
RANK = 64
SAMPLES = 8192
ITERS = 2


step_size = 0.2


def pair_rows(left, right):
    product = left[:, None, :].astype(jnp.float32) * right[None, :, :].astype(jnp.float32)
    return product.reshape(left.shape[0] * right.shape[0], left.shape[1]).astype(jnp.bfloat16)


def contract_last(left, right):
    return lax.dot_general(
        left, right, (((1,), (1,)), ((), ())), preferred_element_type=jnp.float32
    )


def spread(values, width, major):
    place = jnp.arange(width * width, dtype=jnp.int32)
    index = place // width if major else place % width
    pick = (index[None, :] == jnp.arange(width, dtype=jnp.int32)[:, None]).astype(values.dtype)
    return jnp.dot(values, pick, precision=lax.Precision.HIGHEST)


def cumulant_slabs(moments, grams, count, width, row_lo):
    majors, minors, firsts = [], [], []
    for gram in grams:

        def part(first, second, gram=gram):
            return gram[first * width : (first + 1) * width, second * width : (second + 1) * width]

        cov_ab = lax.dynamic_slice_in_dim(part(0, 1), row_lo, count, 0)
        cov_ac = lax.dynamic_slice_in_dim(part(0, 2), row_lo, count, 0)
        cov_ad = lax.dynamic_slice_in_dim(part(0, 3), row_lo, count, 0)
        majors += [cov_ac, part(1, 2)]
        minors += [part(1, 3), cov_ad]
        firsts.append(cov_ab[:, :, None] * part(2, 3).reshape(1, 1, width * width))
    wide_major = spread(jnp.concatenate(majors, axis=0), width, True)
    wide_minor = spread(jnp.concatenate(minors, axis=0), width, False)
    slabs = []
    step = count + width
    for slot, moment in enumerate(moments):
        base = slot * step
        spread_ac = wide_major[base : base + count]
        spread_bc = wide_major[base + count : base + step]
        spread_bd = wide_minor[base : base + width]
        spread_ad = wide_minor[base + width : base + step]
        second_term = spread_ac[:, None, :] * spread_bd[None, :, :]
        third_term = spread_ad[:, None, :] * spread_bc[None, :, :]
        shaped = moment.reshape(count, width, width * width)
        slab = shaped - ((firsts[slot] + second_term) + third_term)
        slabs.append(slab.reshape(count * width, width * width))
    return slabs


def add_cols(total, piece, start):
    old = lax.dynamic_slice_in_dim(total, start, piece.shape[1], 1)
    return lax.dynamic_update_slice_in_dim(total, old + piece, start, 1)


def add_grads(total, kslab, full, ids, row_lo, count, width):
    highest = lax.Precision.HIGHEST
    rank = full.shape[0]
    start_a = ids[0] * width + row_lo
    fac_a = lax.dynamic_slice_in_dim(full, start_a, count, 1)
    fac_b = lax.dynamic_slice_in_dim(full, ids[1] * width, width, 1)
    fac_c = lax.dynamic_slice_in_dim(full, ids[2] * width, width, 1)
    fac_d = lax.dynamic_slice_in_dim(full, ids[3] * width, width, 1)
    upair = (fac_a[:, :, None] * fac_b[:, None, :]).reshape(rank, count * width)
    vpair = (fac_c[:, :, None] * fac_d[:, None, :]).reshape(rank, width * width)
    model = lax.dot_general(upair, vpair, (((0,), (0,)), ((), ())), precision=highest)
    resid = kslab - model
    wmat = lax.dot_general(vpair, resid, (((1,), (1,)), ((), ())), precision=highest).reshape(
        rank, count, width
    )
    zmat = jnp.dot(upair, resid, precision=highest).reshape(rank, width, width)
    total = add_cols(total, jnp.sum(wmat * fac_b[:, None, :], axis=2), start_a)
    total = add_cols(total, jnp.sum(wmat * fac_a[:, :, None], axis=1), ids[1] * width)
    total = add_cols(total, jnp.sum(zmat * fac_d[:, None, :], axis=2), ids[2] * width)
    total = add_cols(total, jnp.sum(zmat * fac_c[:, :, None], axis=1), ids[3] * width)
    return total


def gather_factor(columns):
    stacked = lax.all_gather(columns, "row", axis=0)
    return jnp.transpose(stacked, (1, 0, 2)).reshape(columns.shape[0], -1)


def swap(value, axis, stride):
    size = lax.axis_size(axis)
    return lax.ppermute(value, axis, [(index, index ^ stride) for index in range(size)])


def all_sum(value):
    shape = value.shape
    value = value.reshape(-1, 128)
    upper = lax.axis_index("blk") % 2
    half = value.shape[0] // 2
    low, high = value[:half], value[half:]
    keep = jnp.where(upper == 0, low, high)
    value = keep + swap(jnp.where(upper == 0, high, low), "blk", 1)
    for axis in ("blk", "row"):
        stride = 2 if axis == "blk" else 1
        while stride < lax.axis_size(axis):
            value = value + swap(value, axis, stride)
            stride *= 2
    other = swap(value, "blk", 1)
    value = jnp.where(upper == 0, jnp.concatenate([value, other]), jnp.concatenate([other, value]))
    return value.reshape(shape)


def per_device(samples, blocks, factor):
    width = BLOCK
    row_count = lax.axis_size("row")
    count = width // row_count
    row_lo = lax.axis_index("row") * count
    per_owner = blocks.shape[0] // lax.axis_size("blk")
    mine = lax.dynamic_slice_in_dim(blocks, lax.axis_index("blk") * per_owner, per_owner, 0)
    needed = mine.reshape(-1)
    pairs = width * width
    piece = lax.all_gather(samples, "blk", axis=0, tiled=True)
    pieces = piece.shape[0] // width
    owned = jnp.arange(pieces, dtype=jnp.int32)
    select = (needed[:, None] == owned[None, :]).astype(jnp.bfloat16)
    shaped = piece.reshape(pieces, width, piece.shape[1])
    taken = jnp.einsum("mb,bcs->mcs", select, shaped, preferred_element_type=jnp.float32)
    local = taken.astype(jnp.bfloat16)
    forward = [(index, (index + 1) % row_count) for index in range(row_count)]
    backward = [(index, (index - 1) % row_count) for index in range(row_count)]
    piece_rows = 4 * width
    chunks = [local[4 * slot : 4 * slot + 4] for slot in range(per_owner)]
    moments = [jnp.zeros((count * width, pairs), jnp.float32) for _ in range(per_owner)]
    grams = [jnp.zeros((piece_rows, piece_rows), jnp.float32) for _ in range(per_owner)]
    held = factor
    held_pieces = []
    for step in range(row_count):
        if step + 1 < row_count:
            incoming = [
                lax.ppermute(chunks[slot], "row", forward if slot % 2 == 0 else backward)
                for slot in range(per_owner)
            ]
            held_in = lax.ppermute(held, "row", forward)
        held_pieces.append(held)
        for slot in range(per_owner):
            chunk = chunks[slot]
            left = lax.dynamic_slice_in_dim(chunk[0], row_lo, count, 0)
            pmat = pair_rows(left, chunk[1])
            qmat = pair_rows(chunk[2], chunk[3])
            moments[slot] = moments[slot] + contract_last(pmat, qmat)
            joined = chunk.reshape(piece_rows, chunk.shape[2])
            grams[slot] = grams[slot] + contract_last(joined, joined)
        if step + 1 < row_count:
            chunks, held = incoming, held_in
    slabs = cumulant_slabs(
        [moment / SAMPLES for moment in moments], [gram / SAMPLES for gram in grams], count, width, row_lo
    )
    source = (lax.axis_index("row") - jnp.arange(row_count)) % row_count
    stacked = jnp.stack(held_pieces)[source]
    full = jnp.transpose(stacked, (1, 0, 2)).reshape(factor.shape[0], -1)
    for step in range(ITERS):
        grad = jnp.zeros(full.shape, jnp.float32)
        for slot in range(per_owner):
            grad = add_grads(grad, slabs[slot], full, mine[slot], row_lo, count, width)
        grad = all_sum(grad)
        scale = lax.rsqrt(jnp.mean(grad * grad) + 1e-06)
        full = full + step_size * scale * grad
    col_count = factor.shape[1]
    columns = lax.dynamic_slice_in_dim(full, lax.axis_index("row") * col_count, col_count, 1)
    return (jnp.stack(slabs), columns)


def solution(mesh):
    placed = (P("blk", "row"), P(), P(None, "row"))
    return jax.shard_map(
        per_device,
        mesh=mesh,
        in_specs=placed,
        out_specs=(P("blk", "row", None), P(None, "row")),
        check_vma=False,
    )
```

```python
import jax
import jax.numpy as jnp
from jax import lax
from jax.experimental import pallas as pl
from jax.experimental.pallas import tpu as pltpu
from jax.sharding import PartitionSpec as P

CHANNELS = 1024
BLOCK = 32
RANK = 64
SAMPLES = 8192
ITERS = 2


step_size = 0.2


def pair_rows(left, right):
    product = left[:, None, :].astype(jnp.float32) * right[None, :, :].astype(jnp.float32)
    return product.reshape(left.shape[0] * right.shape[0], left.shape[1]).astype(jnp.bfloat16)


def contract_last(left, right):
    return lax.dot_general(
        left, right, (((1,), (1,)), ((), ())), preferred_element_type=jnp.float32
    )


def spread(values, width, major):
    place = jnp.arange(width * width, dtype=jnp.int32)
    index = place // width if major else place % width
    pick = (index[None, :] == jnp.arange(width, dtype=jnp.int32)[:, None]).astype(values.dtype)
    return jnp.dot(values, pick, precision=lax.Precision.HIGHEST)


def cumulant_slab(moment, gram, count, width, row_lo):
    def part(first, second):
        return gram[first * width : (first + 1) * width, second * width : (second + 1) * width]

    cov_ab = lax.dynamic_slice_in_dim(part(0, 1), row_lo, count, 0)
    cov_ac = lax.dynamic_slice_in_dim(part(0, 2), row_lo, count, 0)
    cov_ad = lax.dynamic_slice_in_dim(part(0, 3), row_lo, count, 0)
    cov_cd = part(2, 3)
    cov_bd = part(1, 3)
    cov_bc = part(1, 2)
    first_term = cov_ab[:, :, None] * cov_cd.reshape(1, 1, width * width)
    second_term = spread(cov_ac, width, True)[:, None, :] * spread(cov_bd, width, False)[None, :, :]
    third_term = spread(cov_ad, width, False)[:, None, :] * spread(cov_bc, width, True)[None, :, :]
    shaped = moment.reshape(count, width, width * width)
    slab = shaped - ((first_term + second_term) + third_term)
    return slab.reshape(count * width, width * width)


def add_cols(total, piece, start):
    old = lax.dynamic_slice_in_dim(total, start, piece.shape[1], 1)
    return lax.dynamic_update_slice_in_dim(total, old + piece, start, 1)


def add_grads(total, kslab, full, ids, row_lo, count, width):
    highest = lax.Precision.HIGHEST
    rank = full.shape[0]
    start_a = ids[0] * width + row_lo
    fac_a = lax.dynamic_slice_in_dim(full, start_a, count, 1)
    fac_b = lax.dynamic_slice_in_dim(full, ids[1] * width, width, 1)
    fac_c = lax.dynamic_slice_in_dim(full, ids[2] * width, width, 1)
    fac_d = lax.dynamic_slice_in_dim(full, ids[3] * width, width, 1)
    upair = (fac_a[:, :, None] * fac_b[:, None, :]).reshape(rank, count * width)
    vpair = (fac_c[:, :, None] * fac_d[:, None, :]).reshape(rank, width * width)
    model = lax.dot_general(upair, vpair, (((0,), (0,)), ((), ())), precision=highest)
    resid = kslab - model
    wmat = lax.dot_general(vpair, resid, (((1,), (1,)), ((), ())), precision=highest).reshape(
        rank, count, width
    )
    zmat = jnp.dot(upair, resid, precision=highest).reshape(rank, width, width)
    total = add_cols(total, jnp.sum(wmat * fac_b[:, None, :], axis=2), start_a)
    total = add_cols(total, jnp.sum(wmat * fac_a[:, :, None], axis=1), ids[1] * width)
    total = add_cols(total, jnp.sum(zmat * fac_d[:, None, :], axis=2), ids[2] * width)
    total = add_cols(total, jnp.sum(zmat * fac_c[:, :, None], axis=1), ids[3] * width)
    return total


def moment_kernel(left_ref, chunk_ref, moment_ref, gram_ref, moment_out, gram_out, qmat_ref, pmat_ref):
    width = chunk_ref.shape[1]
    count = left_ref.shape[0]
    right = chunk_ref[1].astype(jnp.float32)
    for i in range(count):
        pmat_ref[pl.ds(i * width, width), :] = (left_ref[pl.ds(i, 1), :].astype(jnp.float32) * right).astype(jnp.bfloat16)
    fourth = chunk_ref[3].astype(jnp.float32)

    def build(group, carry):
        low = pl.multiple_of(group * 8, 8)
        thirds = chunk_ref[2, pl.ds(low, 8), :].astype(jnp.float32)
        for row in range(8):
            start = pl.multiple_of((low + row) * width, width)
            qmat_ref[pl.ds(start, width), :] = (thirds[row : row + 1, :] * fourth).astype(jnp.bfloat16)
        return carry

    lax.fori_loop(0, width // 8, build, 0)
    dims = (((1,), (1,)), ((), ()))
    moment_out[...] = moment_ref[...] + lax.dot_general(
        pmat_ref[...], qmat_ref[...], dims, preferred_element_type=jnp.float32)
    joined = chunk_ref[...].reshape(4 * width, chunk_ref.shape[2])
    gram_out[...] = gram_ref[...] + lax.dot_general(joined, joined, dims, preferred_element_type=jnp.float32)

def moment_step(left, chunk, moment, gram):
    width = chunk.shape[1]
    samples = chunk.shape[2]
    spec = pl.BlockSpec(memory_space=pltpu.MemorySpace.VMEM)
    return pl.pallas_call(
        moment_kernel,
        out_shape=(jax.ShapeDtypeStruct(moment.shape, jnp.float32), jax.ShapeDtypeStruct(gram.shape, jnp.float32)),
        in_specs=[spec] * 4,
        out_specs=(spec, spec),
        scratch_shapes=[pltpu.VMEM((width * width, samples), jnp.bfloat16),
                        pltpu.VMEM((left.shape[0] * width, samples), jnp.bfloat16)],
        input_output_aliases={2: 0, 3: 1},
    )(left, chunk, moment, gram)


def gather_factor(columns):
    stacked = lax.all_gather(columns, "row", axis=0)
    return jnp.transpose(stacked, (1, 0, 2)).reshape(columns.shape[0], -1)


def swap(value, axis, stride):
    size = lax.axis_size(axis)
    return lax.ppermute(value, axis, [(index, index ^ stride) for index in range(size)])


def all_sum(value):
    shape = value.shape
    value = value.reshape(-1, 128)
    upper = lax.axis_index("blk") % 2
    half = value.shape[0] // 2
    low, high = value[:half], value[half:]
    keep = jnp.where(upper == 0, low, high)
    value = keep + swap(jnp.where(upper == 0, high, low), "blk", 1)
    for axis in ("blk", "row"):
        stride = 2 if axis == "blk" else 1
        while stride < lax.axis_size(axis):
            value = value + swap(value, axis, stride)
            stride *= 2
    other = swap(value, "blk", 1)
    value = jnp.where(upper == 0, jnp.concatenate([value, other]), jnp.concatenate([other, value]))
    return value.reshape(shape)


def per_device(samples, blocks, factor):
    width = BLOCK
    row_count = lax.axis_size("row")
    count = width // row_count
    row_lo = lax.axis_index("row") * count
    per_owner = blocks.shape[0] // lax.axis_size("blk")
    mine = lax.dynamic_slice_in_dim(blocks, lax.axis_index("blk") * per_owner, per_owner, 0)
    needed = mine.reshape(-1)
    pairs = width * width
    piece = lax.all_gather(samples, "blk", axis=0, tiled=True)
    pieces = piece.shape[0] // width
    owned = jnp.arange(pieces, dtype=jnp.int32)
    select = (needed[:, None] == owned[None, :]).astype(jnp.bfloat16)
    shaped = piece.reshape(pieces, width, piece.shape[1])
    taken = jnp.einsum("mb,bcs->mcs", select, shaped, preferred_element_type=jnp.float32)
    local = taken.astype(jnp.bfloat16)
    forward = [(index, (index + 1) % row_count) for index in range(row_count)]
    backward = [(index, (index - 1) % row_count) for index in range(row_count)]
    piece_rows = 4 * width
    chunks = [local[4 * slot : 4 * slot + 4] for slot in range(per_owner)]
    moments = [jnp.zeros((count * width, pairs), jnp.float32) for _ in range(per_owner)]
    grams = [jnp.zeros((piece_rows, piece_rows), jnp.float32) for _ in range(per_owner)]
    held = factor
    held_pieces = []
    for step in range(row_count):
        if step + 1 < row_count:
            incoming = [
                lax.ppermute(chunks[slot], "row", forward if slot % 2 == 0 else backward)
                for slot in range(per_owner)
            ]
            held_in = lax.ppermute(held, "row", forward)
        held_pieces.append(held)
        for slot in range(per_owner):
            chunk = chunks[slot]
            left = lax.dynamic_slice_in_dim(chunk[0], row_lo, count, 0)
            moments[slot], grams[slot] = moment_step(left, chunk, moments[slot], grams[slot])
        if step + 1 < row_count:
            chunks, held = incoming, held_in
    slabs = []
    for slot in range(per_owner):
        moment = moments[slot] / SAMPLES
        gram = grams[slot] / SAMPLES
        slabs.append(cumulant_slab(moment, gram, count, width, row_lo))
    source = (lax.axis_index("row") - jnp.arange(row_count)) % row_count
    stacked = jnp.stack(held_pieces)[source]
    full = jnp.transpose(stacked, (1, 0, 2)).reshape(factor.shape[0], -1)
    for step in range(ITERS):
        grad = jnp.zeros(full.shape, jnp.float32)
        for slot in range(per_owner):
            grad = add_grads(grad, slabs[slot], full, mine[slot], row_lo, count, width)
        grad = all_sum(grad)
        scale = lax.rsqrt(jnp.mean(grad * grad) + 1e-06)
        full = full + step_size * scale * grad
    col_count = factor.shape[1]
    columns = lax.dynamic_slice_in_dim(full, lax.axis_index("row") * col_count, col_count, 1)
    return (jnp.stack(slabs), columns)


def solution(mesh):
    placed = (P("blk", "row"), P(), P(None, "row"))
    return jax.shard_map(
        per_device,
        mesh=mesh,
        in_specs=placed,
        out_specs=(P("blk", "row", None), P(None, "row")),
        check_vma=False,
    )
```

```python
import jax
import jax.numpy as jnp
from jax import lax
from jax.experimental import pallas as pl
from jax.experimental.pallas import tpu as pltpu
from jax.sharding import PartitionSpec as P

CHANNELS = 1024
BLOCK = 32
RANK = 64
SAMPLES = 8192
ITERS = 2


step_size = 0.2


def pair_rows(left, right):
    product = left[:, None, :].astype(jnp.float32) * right[None, :, :].astype(jnp.float32)
    return product.reshape(left.shape[0] * right.shape[0], left.shape[1]).astype(jnp.bfloat16)


def contract_last(left, right):
    return lax.dot_general(
        left, right, (((1,), (1,)), ((), ())), preferred_element_type=jnp.float32
    )


def spread(values, width, major):
    place = jnp.arange(width * width, dtype=jnp.int32)
    index = place // width if major else place % width
    pick = (index[None, :] == jnp.arange(width, dtype=jnp.int32)[:, None]).astype(values.dtype)
    return jnp.dot(values, pick, precision=lax.Precision.HIGHEST)


def cumulant_slab(moment, gram, count, width, row_lo):
    def part(first, second):
        return gram[first * width : (first + 1) * width, second * width : (second + 1) * width]

    cov_ab = lax.dynamic_slice_in_dim(part(0, 1), row_lo, count, 0)
    cov_ac = lax.dynamic_slice_in_dim(part(0, 2), row_lo, count, 0)
    cov_ad = lax.dynamic_slice_in_dim(part(0, 3), row_lo, count, 0)
    cov_cd = part(2, 3)
    cov_bd = part(1, 3)
    cov_bc = part(1, 2)
    first_term = cov_ab[:, :, None] * cov_cd.reshape(1, 1, width * width)
    second_term = spread(cov_ac, width, True)[:, None, :] * spread(cov_bd, width, False)[None, :, :]
    third_term = spread(cov_ad, width, False)[:, None, :] * spread(cov_bc, width, True)[None, :, :]
    shaped = moment.reshape(count, width, width * width)
    slab = shaped - ((first_term + second_term) + third_term)
    return slab.reshape(count * width, width * width)


def add_cols(total, piece, start):
    old = lax.dynamic_slice_in_dim(total, start, piece.shape[1], 1)
    return lax.dynamic_update_slice_in_dim(total, old + piece, start, 1)


def add_grads(total, kslab, full, ids, row_lo, count, width):
    highest = lax.Precision.HIGHEST
    rank = full.shape[0]
    start_a = ids[0] * width + row_lo
    fac_a = lax.dynamic_slice_in_dim(full, start_a, count, 1)
    fac_b = lax.dynamic_slice_in_dim(full, ids[1] * width, width, 1)
    fac_c = lax.dynamic_slice_in_dim(full, ids[2] * width, width, 1)
    fac_d = lax.dynamic_slice_in_dim(full, ids[3] * width, width, 1)
    upair = (fac_a[:, :, None] * fac_b[:, None, :]).reshape(rank, count * width)
    vpair = (fac_c[:, :, None] * fac_d[:, None, :]).reshape(rank, width * width)
    model = lax.dot_general(upair, vpair, (((0,), (0,)), ((), ())), precision=highest)
    resid = kslab - model
    wmat = lax.dot_general(vpair, resid, (((1,), (1,)), ((), ())), precision=highest).reshape(
        rank, count, width
    )
    zmat = jnp.dot(upair, resid, precision=highest).reshape(rank, width, width)
    total = add_cols(total, jnp.sum(wmat * fac_b[:, None, :], axis=2), start_a)
    total = add_cols(total, jnp.sum(wmat * fac_a[:, :, None], axis=1), ids[1] * width)
    total = add_cols(total, jnp.sum(zmat * fac_d[:, None, :], axis=2), ids[2] * width)
    total = add_cols(total, jnp.sum(zmat * fac_c[:, :, None], axis=1), ids[3] * width)
    return total


def moment_kernel(left_ref, chunk_ref, moment_ref, gram_ref, moment_out, gram_out, qmat_ref, pmat_ref):
    width = chunk_ref.shape[1]
    count = left_ref.shape[0]
    right = chunk_ref[1].astype(jnp.float32)
    for i in range(count):
        pmat_ref[pl.ds(i * width, width), :] = (left_ref[pl.ds(i, 1), :].astype(jnp.float32) * right).astype(jnp.bfloat16)
    fourth = chunk_ref[3].astype(jnp.float32)

    def build(group, carry):
        low = pl.multiple_of(group * 8, 8)
        thirds = chunk_ref[2, pl.ds(low, 8), :].astype(jnp.float32)
        for row in range(8):
            start = pl.multiple_of((low + row) * width, width)
            qmat_ref[pl.ds(start, width), :] = (thirds[row : row + 1, :] * fourth).astype(jnp.bfloat16)
        return carry

    lax.fori_loop(0, width // 8, build, 0)
    dims = (((1,), (1,)), ((), ()))
    moment_out[...] = moment_ref[...] + lax.dot_general(
        pmat_ref[...], qmat_ref[...], dims, preferred_element_type=jnp.float32)
    joined = chunk_ref[...].reshape(4 * width, chunk_ref.shape[2])
    gram_out[...] = gram_ref[...] + lax.dot_general(joined, joined, dims, preferred_element_type=jnp.float32)

def moment_step(left, chunk, moment, gram):
    width = chunk.shape[1]
    samples = chunk.shape[2]
    spec = pl.BlockSpec(memory_space=pltpu.MemorySpace.VMEM)
    return pl.pallas_call(
        moment_kernel,
        out_shape=(jax.ShapeDtypeStruct(moment.shape, jnp.float32), jax.ShapeDtypeStruct(gram.shape, jnp.float32)),
        in_specs=[spec] * 4,
        out_specs=(spec, spec),
        scratch_shapes=[pltpu.VMEM((width * width, samples), jnp.bfloat16),
                        pltpu.VMEM((left.shape[0] * width, samples), jnp.bfloat16)],
        input_output_aliases={2: 0, 3: 1},
        cost_estimate=pl.CostEstimate(
            flops=2 * moment.size * samples + 2 * gram.size * samples + 3 * width * width * samples,
            transcendentals=0,
            bytes_accessed=2 * (moment.size + gram.size) * 4 + chunk.size * 2 + left.size * 2,
        ),
    )(left, chunk, moment, gram)


def gather_factor(columns):
    stacked = lax.all_gather(columns, "row", axis=0)
    return jnp.transpose(stacked, (1, 0, 2)).reshape(columns.shape[0], -1)


def swap(value, axis, stride):
    size = lax.axis_size(axis)
    return lax.ppermute(value, axis, [(index, index ^ stride) for index in range(size)])


def all_sum(value):
    shape = value.shape
    value = value.reshape(-1, 128)
    upper = lax.axis_index("blk") % 2
    half = value.shape[0] // 2
    low, high = value[:half], value[half:]
    keep = jnp.where(upper == 0, low, high)
    value = keep + swap(jnp.where(upper == 0, high, low), "blk", 1)
    for axis in ("blk", "row"):
        stride = 2 if axis == "blk" else 1
        while stride < lax.axis_size(axis):
            value = value + swap(value, axis, stride)
            stride *= 2
    other = swap(value, "blk", 1)
    value = jnp.where(upper == 0, jnp.concatenate([value, other]), jnp.concatenate([other, value]))
    return value.reshape(shape)


def per_device(samples, blocks, factor):
    width = BLOCK
    row_count = lax.axis_size("row")
    count = width // row_count
    row_lo = lax.axis_index("row") * count
    per_owner = blocks.shape[0] // lax.axis_size("blk")
    mine = lax.dynamic_slice_in_dim(blocks, lax.axis_index("blk") * per_owner, per_owner, 0)
    needed = mine.reshape(-1)
    pairs = width * width
    piece = lax.all_gather(samples, "blk", axis=0, tiled=True)
    pieces = piece.shape[0] // width
    owned = jnp.arange(pieces, dtype=jnp.int32)
    select = (needed[:, None] == owned[None, :]).astype(jnp.bfloat16)
    shaped = piece.reshape(pieces, width, piece.shape[1])
    taken = jnp.einsum("mb,bcs->mcs", select, shaped, preferred_element_type=jnp.float32)
    local = taken.astype(jnp.bfloat16)
    forward = [(index, (index + 1) % row_count) for index in range(row_count)]
    backward = [(index, (index - 1) % row_count) for index in range(row_count)]
    piece_rows = 4 * width
    chunks = [local[4 * slot : 4 * slot + 4] for slot in range(per_owner)]
    moments = [jnp.zeros((count * width, pairs), jnp.float32) for _ in range(per_owner)]
    grams = [jnp.zeros((piece_rows, piece_rows), jnp.float32) for _ in range(per_owner)]
    held = factor
    held_pieces = []
    for step in range(row_count):
        if step + 1 < row_count:
            incoming = [
                lax.ppermute(chunks[slot], "row", forward if slot % 2 == 0 else backward)
                for slot in range(per_owner)
            ]
            held_in = lax.ppermute(held, "row", forward)
        held_pieces.append(held)
        for slot in range(per_owner):
            chunk = chunks[slot]
            left = lax.dynamic_slice_in_dim(chunk[0], row_lo, count, 0)
            moments[slot], grams[slot] = moment_step(left, chunk, moments[slot], grams[slot])
        if step + 1 < row_count:
            chunks, held = incoming, held_in
    slabs = []
    for slot in range(per_owner):
        moment = moments[slot] / SAMPLES
        gram = grams[slot] / SAMPLES
        slabs.append(cumulant_slab(moment, gram, count, width, row_lo))
    source = (lax.axis_index("row") - jnp.arange(row_count)) % row_count
    stacked = jnp.stack(held_pieces)[source]
    full = jnp.transpose(stacked, (1, 0, 2)).reshape(factor.shape[0], -1)
    for step in range(ITERS):
        grad = jnp.zeros(full.shape, jnp.float32)
        for slot in range(per_owner):
            grad = add_grads(grad, slabs[slot], full, mine[slot], row_lo, count, width)
        grad = all_sum(grad)
        scale = lax.rsqrt(jnp.mean(grad * grad) + 1e-06)
        full = full + step_size * scale * grad
    col_count = factor.shape[1]
    columns = lax.dynamic_slice_in_dim(full, lax.axis_index("row") * col_count, col_count, 1)
    return (jnp.stack(slabs), columns)


def solution(mesh):
    placed = (P("blk", "row"), P(), P(None, "row"))
    return jax.shard_map(
        per_device,
        mesh=mesh,
        in_specs=placed,
        out_specs=(P("blk", "row", None), P(None, "row")),
        check_vma=False,
    )
```

```python
import jax
import jax.numpy as jnp
from jax import lax
from jax.experimental import pallas as pl
from jax.experimental.pallas import tpu as pltpu
from jax.sharding import PartitionSpec as P

CHANNELS = 1024
BLOCK = 32
RANK = 64
SAMPLES = 8192
ITERS = 2


step_size = 0.2


def pair_rows(left, right):
    product = left[:, None, :].astype(jnp.float32) * right[None, :, :].astype(jnp.float32)
    return product.reshape(left.shape[0] * right.shape[0], left.shape[1]).astype(jnp.bfloat16)


def contract_last(left, right):
    return lax.dot_general(
        left, right, (((1,), (1,)), ((), ())), preferred_element_type=jnp.float32
    )


def spread(values, width, major):
    place = jnp.arange(width * width, dtype=jnp.int32)
    index = place // width if major else place % width
    pick = (index[None, :] == jnp.arange(width, dtype=jnp.int32)[:, None]).astype(values.dtype)
    return jnp.dot(values, pick, precision=lax.Precision.HIGHEST)


def cumulant_slab(moment, gram, count, width, row_lo):
    def part(first, second):
        return gram[first * width : (first + 1) * width, second * width : (second + 1) * width]

    cov_ab = lax.dynamic_slice_in_dim(part(0, 1), row_lo, count, 0)
    cov_ac = lax.dynamic_slice_in_dim(part(0, 2), row_lo, count, 0)
    cov_ad = lax.dynamic_slice_in_dim(part(0, 3), row_lo, count, 0)
    cov_cd = part(2, 3)
    cov_bd = part(1, 3)
    cov_bc = part(1, 2)
    first_term = cov_ab[:, :, None] * cov_cd.reshape(1, 1, width * width)
    second_term = spread(cov_ac, width, True)[:, None, :] * spread(cov_bd, width, False)[None, :, :]
    third_term = spread(cov_ad, width, False)[:, None, :] * spread(cov_bc, width, True)[None, :, :]
    shaped = moment.reshape(count, width, width * width)
    slab = shaped - ((first_term + second_term) + third_term)
    return slab.reshape(count * width, width * width)


def add_cols(total, piece, start):
    old = lax.dynamic_slice_in_dim(total, start, piece.shape[1], 1)
    return lax.dynamic_update_slice_in_dim(total, old + piece, start, 1)


def add_grads(total, kslab, full, ids, row_lo, count, width):
    highest = lax.Precision.HIGHEST
    rank = full.shape[0]
    start_a = ids[0] * width + row_lo
    fac_a = lax.dynamic_slice_in_dim(full, start_a, count, 1)
    fac_b = lax.dynamic_slice_in_dim(full, ids[1] * width, width, 1)
    fac_c = lax.dynamic_slice_in_dim(full, ids[2] * width, width, 1)
    fac_d = lax.dynamic_slice_in_dim(full, ids[3] * width, width, 1)
    upair = (fac_a[:, :, None] * fac_b[:, None, :]).reshape(rank, count * width)
    vpair = (fac_c[:, :, None] * fac_d[:, None, :]).reshape(rank, width * width)
    model = lax.dot_general(upair, vpair, (((0,), (0,)), ((), ())), precision=highest)
    resid = kslab - model
    wmat = lax.dot_general(vpair, resid, (((1,), (1,)), ((), ())), precision=highest).reshape(
        rank, count, width
    )
    zmat = jnp.dot(upair, resid, precision=highest).reshape(rank, width, width)
    total = add_cols(total, jnp.sum(wmat * fac_b[:, None, :], axis=2), start_a)
    total = add_cols(total, jnp.sum(wmat * fac_a[:, :, None], axis=1), ids[1] * width)
    total = add_cols(total, jnp.sum(zmat * fac_d[:, None, :], axis=2), ids[2] * width)
    total = add_cols(total, jnp.sum(zmat * fac_c[:, :, None], axis=1), ids[3] * width)
    return total


def moment_kernel(left_ref, chunk_ref, moment_ref, gram_ref, moment_out, gram_out, qmat_ref, pmat_ref):
    width = chunk_ref.shape[1]
    count = left_ref.shape[0]
    right = chunk_ref[1].astype(jnp.float32)
    for i in range(count):
        pmat_ref[pl.ds(i * width, width), :] = (left_ref[pl.ds(i, 1), :].astype(jnp.float32) * right).astype(jnp.bfloat16)
    fourth = chunk_ref[3].astype(jnp.float32)

    def build(group, carry):
        low = pl.multiple_of(group * 8, 8)
        thirds = chunk_ref[2, pl.ds(low, 8), :].astype(jnp.float32)
        for row in range(8):
            start = pl.multiple_of((low + row) * width, width)
            qmat_ref[pl.ds(start, width), :] = (thirds[row : row + 1, :] * fourth).astype(jnp.bfloat16)
        return carry

    lax.fori_loop(0, width // 8, build, 0)
    dims = (((1,), (1,)), ((), ()))
    moment_out[...] = moment_ref[...] + lax.dot_general(
        pmat_ref[...], qmat_ref[...], dims, preferred_element_type=jnp.float32)
    joined = chunk_ref[...].reshape(4 * width, chunk_ref.shape[2])
    gram_out[...] = gram_ref[...] + lax.dot_general(joined, joined, dims, preferred_element_type=jnp.float32)

def moment_step(left, chunk, moment, gram):
    width = chunk.shape[1]
    samples = chunk.shape[2]
    spec = pl.BlockSpec(memory_space=pltpu.MemorySpace.VMEM)
    return pl.pallas_call(
        moment_kernel,
        out_shape=(jax.ShapeDtypeStruct(moment.shape, jnp.float32), jax.ShapeDtypeStruct(gram.shape, jnp.float32)),
        in_specs=[spec] * 4,
        out_specs=(spec, spec),
        scratch_shapes=[pltpu.VMEM((width * width, samples), jnp.bfloat16),
                        pltpu.VMEM((left.shape[0] * width, samples), jnp.bfloat16)],
        input_output_aliases={2: 0, 3: 1},
        cost_estimate=pl.CostEstimate(
            flops=2 * moment.size * samples + 2 * gram.size * samples + 3 * width * width * samples,
            transcendentals=0,
            bytes_accessed=2 * (moment.size + gram.size) * 4 + chunk.size * 2 + left.size * 2,
        ),
    )(left, chunk, moment, gram)


def gather_factor(columns):
    stacked = lax.all_gather(columns, "row", axis=0)
    return jnp.transpose(stacked, (1, 0, 2)).reshape(columns.shape[0], -1)


def swap(value, axis, stride):
    size = lax.axis_size(axis)
    return lax.ppermute(value, axis, [(index, index ^ stride) for index in range(size)])


def group_sum(value, axis, stride):
    place = (lax.axis_index(axis) // stride) % 4
    received = [value] + [swap(value, axis, stride * member) for member in range(1, 4)]
    ordered = []
    for member in range(4):
        held = received[0]
        for offset in range(1, 4):
            held = jnp.where(jnp.bitwise_xor(place, member) == offset, received[offset], held)
        ordered.append(held)
    return (ordered[0] + ordered[1]) + (ordered[2] + ordered[3])


def all_sum(value):
    shape = value.shape
    value = value.reshape(-1, 128)
    upper = lax.axis_index("blk") % 2
    half = value.shape[0] // 2
    low, high = value[:half], value[half:]
    keep = jnp.where(upper == 0, low, high)
    value = keep + swap(jnp.where(upper == 0, high, low), "blk", 1)
    value = group_sum(value, "blk", 2)
    value = group_sum(value, "blk", 8)
    value = group_sum(value, "row", 1)
    stride = 4
    while stride < lax.axis_size("row"):
        value = value + swap(value, "row", stride)
        stride *= 2
    other = swap(value, "blk", 1)
    value = jnp.where(upper == 0, jnp.concatenate([value, other]), jnp.concatenate([other, value]))
    return value.reshape(shape)


def per_device(samples, blocks, factor):
    width = BLOCK
    row_count = lax.axis_size("row")
    count = width // row_count
    row_lo = lax.axis_index("row") * count
    per_owner = blocks.shape[0] // lax.axis_size("blk")
    mine = lax.dynamic_slice_in_dim(blocks, lax.axis_index("blk") * per_owner, per_owner, 0)
    needed = mine.reshape(-1)
    pairs = width * width
    piece = lax.all_gather(samples, "blk", axis=0, tiled=True)
    pieces = piece.shape[0] // width
    owned = jnp.arange(pieces, dtype=jnp.int32)
    select = (needed[:, None] == owned[None, :]).astype(jnp.bfloat16)
    shaped = piece.reshape(pieces, width, piece.shape[1])
    taken = jnp.einsum("mb,bcs->mcs", select, shaped, preferred_element_type=jnp.float32)
    local = taken.astype(jnp.bfloat16)
    forward = [(index, (index + 1) % row_count) for index in range(row_count)]
    backward = [(index, (index - 1) % row_count) for index in range(row_count)]
    piece_rows = 4 * width
    chunks = [local[4 * slot : 4 * slot + 4] for slot in range(per_owner)]
    moments = [jnp.zeros((count * width, pairs), jnp.float32) for _ in range(per_owner)]
    grams = [jnp.zeros((piece_rows, piece_rows), jnp.float32) for _ in range(per_owner)]
    held = factor
    held_pieces = []
    for step in range(row_count):
        if step + 1 < row_count:
            incoming = [
                lax.ppermute(chunks[slot], "row", forward if slot % 2 == 0 else backward)
                for slot in range(per_owner)
            ]
            held_in = lax.ppermute(held, "row", forward)
        held_pieces.append(held)
        for slot in range(per_owner):
            chunk = chunks[slot]
            left = lax.dynamic_slice_in_dim(chunk[0], row_lo, count, 0)
            moments[slot], grams[slot] = moment_step(left, chunk, moments[slot], grams[slot])
        if step + 1 < row_count:
            chunks, held = incoming, held_in
    slabs = []
    for slot in range(per_owner):
        moment = moments[slot] / SAMPLES
        gram = grams[slot] / SAMPLES
        slabs.append(cumulant_slab(moment, gram, count, width, row_lo))
    source = (lax.axis_index("row") - jnp.arange(row_count)) % row_count
    stacked = jnp.stack(held_pieces)[source]
    full = jnp.transpose(stacked, (1, 0, 2)).reshape(factor.shape[0], -1)
    for step in range(ITERS):
        grad = jnp.zeros(full.shape, jnp.float32)
        for slot in range(per_owner):
            grad = add_grads(grad, slabs[slot], full, mine[slot], row_lo, count, width)
        grad = all_sum(grad)
        scale = lax.rsqrt(jnp.mean(grad * grad) + 1e-06)
        full = full + step_size * scale * grad
    col_count = factor.shape[1]
    columns = lax.dynamic_slice_in_dim(full, lax.axis_index("row") * col_count, col_count, 1)
    return (jnp.stack(slabs), columns)


def solution(mesh):
    placed = (P("blk", "row"), P(), P(None, "row"))
    return jax.shard_map(
        per_device,
        mesh=mesh,
        in_specs=placed,
        out_specs=(P("blk", "row", None), P(None, "row")),
        check_vma=False,
    )
```

```python
import jax
import jax.numpy as jnp
from jax import lax
from jax.experimental import pallas as pl
from jax.experimental.pallas import tpu as pltpu
from jax.sharding import PartitionSpec as P

CHANNELS = 1024
BLOCK = 32
RANK = 64
SAMPLES = 8192
ITERS = 2


step_size = 0.2


def pair_rows(left, right):
    product = left[:, None, :].astype(jnp.float32) * right[None, :, :].astype(jnp.float32)
    return product.reshape(left.shape[0] * right.shape[0], left.shape[1]).astype(jnp.bfloat16)


def contract_last(left, right):
    return lax.dot_general(
        left, right, (((1,), (1,)), ((), ())), preferred_element_type=jnp.float32
    )


def spread(values, width, major):
    place = jnp.arange(width * width, dtype=jnp.int32)
    index = place // width if major else place % width
    pick = (index[None, :] == jnp.arange(width, dtype=jnp.int32)[:, None]).astype(values.dtype)
    return jnp.dot(values, pick, precision=lax.Precision.HIGHEST)


def cumulant_slab(moment, gram, count, width, row_lo):
    def part(first, second):
        return gram[first * width : (first + 1) * width, second * width : (second + 1) * width]

    cov_ab = lax.dynamic_slice_in_dim(part(0, 1), row_lo, count, 0)
    cov_ac = lax.dynamic_slice_in_dim(part(0, 2), row_lo, count, 0)
    cov_ad = lax.dynamic_slice_in_dim(part(0, 3), row_lo, count, 0)
    cov_cd = part(2, 3)
    cov_bd = part(1, 3)
    cov_bc = part(1, 2)
    first_term = cov_ab[:, :, None] * cov_cd.reshape(1, 1, width * width)
    second_term = spread(cov_ac, width, True)[:, None, :] * spread(cov_bd, width, False)[None, :, :]
    third_term = spread(cov_ad, width, False)[:, None, :] * spread(cov_bc, width, True)[None, :, :]
    shaped = moment.reshape(count, width, width * width)
    slab = shaped - ((first_term + second_term) + third_term)
    return slab.reshape(count * width, width * width)


def add_cols(total, piece, start):
    old = lax.dynamic_slice_in_dim(total, start, piece.shape[1], 1)
    return lax.dynamic_update_slice_in_dim(total, old + piece, start, 1)


def add_grads(total, kslab, full, ids, row_lo, count, width):
    highest = lax.Precision.HIGHEST
    rank = full.shape[0]
    start_a = ids[0] * width + row_lo
    fac_a = lax.dynamic_slice_in_dim(full, start_a, count, 1)
    fac_b = lax.dynamic_slice_in_dim(full, ids[1] * width, width, 1)
    fac_c = lax.dynamic_slice_in_dim(full, ids[2] * width, width, 1)
    fac_d = lax.dynamic_slice_in_dim(full, ids[3] * width, width, 1)
    upair = (fac_a[:, :, None] * fac_b[:, None, :]).reshape(rank, count * width)
    vpair = (fac_c[:, :, None] * fac_d[:, None, :]).reshape(rank, width * width)
    model = lax.dot_general(upair, vpair, (((0,), (0,)), ((), ())), precision=highest)
    resid = kslab - model
    wmat = lax.dot_general(vpair, resid, (((1,), (1,)), ((), ())), precision=highest).reshape(
        rank, count, width
    )
    zmat = jnp.dot(upair, resid, precision=highest).reshape(rank, width, width)
    total = add_cols(total, jnp.sum(wmat * fac_b[:, None, :], axis=2), start_a)
    total = add_cols(total, jnp.sum(wmat * fac_a[:, :, None], axis=1), ids[1] * width)
    total = add_cols(total, jnp.sum(zmat * fac_d[:, None, :], axis=2), ids[2] * width)
    total = add_cols(total, jnp.sum(zmat * fac_c[:, :, None], axis=1), ids[3] * width)
    return total


def moment_kernel(left_ref, chunk_ref, moment_ref, gram_ref, moment_out, gram_out, qmat_ref, pmat_ref):
    width = chunk_ref.shape[1]
    count = left_ref.shape[0]
    right = chunk_ref[1].astype(jnp.float32)
    for i in range(count):
        pmat_ref[pl.ds(i * width, width), :] = (left_ref[pl.ds(i, 1), :].astype(jnp.float32) * right).astype(jnp.bfloat16)
    fourth = chunk_ref[3].astype(jnp.float32)

    def build(group, carry):
        low = pl.multiple_of(group * 8, 8)
        thirds = chunk_ref[2, pl.ds(low, 8), :].astype(jnp.float32)
        for row in range(8):
            start = pl.multiple_of((low + row) * width, width)
            qmat_ref[pl.ds(start, width), :] = (thirds[row : row + 1, :] * fourth).astype(jnp.bfloat16)
        return carry

    lax.fori_loop(0, width // 8, build, 0)
    dims = (((1,), (1,)), ((), ()))
    moment_out[...] = moment_ref[...] + lax.dot_general(
        pmat_ref[...], qmat_ref[...], dims, preferred_element_type=jnp.float32)
    joined = chunk_ref[...].reshape(4 * width, chunk_ref.shape[2])
    gram_out[...] = gram_ref[...] + lax.dot_general(joined, joined, dims, preferred_element_type=jnp.float32)

def moment_step(left, chunk, moment, gram):
    width = chunk.shape[1]
    samples = chunk.shape[2]
    spec = pl.BlockSpec(memory_space=pltpu.MemorySpace.VMEM)
    return pl.pallas_call(
        moment_kernel,
        out_shape=(jax.ShapeDtypeStruct(moment.shape, jnp.float32), jax.ShapeDtypeStruct(gram.shape, jnp.float32)),
        in_specs=[spec] * 4,
        out_specs=(spec, spec),
        scratch_shapes=[pltpu.VMEM((width * width, samples), jnp.bfloat16),
                        pltpu.VMEM((left.shape[0] * width, samples), jnp.bfloat16)],
        input_output_aliases={2: 0, 3: 1},
        cost_estimate=pl.CostEstimate(
            flops=2 * moment.size * samples + 2 * gram.size * samples + 3 * width * width * samples,
            transcendentals=0,
            bytes_accessed=2 * (moment.size + gram.size) * 4 + chunk.size * 2 + left.size * 2,
        ),
    )(left, chunk, moment, gram)


def gather_factor(columns):
    stacked = lax.all_gather(columns, "row", axis=0)
    return jnp.transpose(stacked, (1, 0, 2)).reshape(columns.shape[0], -1)


def swap(value, axis, stride):
    size = lax.axis_size(axis)
    return lax.ppermute(value, axis, [(index, index ^ stride) for index in range(size)])


def group_sum(value, axis, stride):
    place = (lax.axis_index(axis) // stride) % 4
    received = [value] + [swap(value, axis, stride * member) for member in range(1, 4)]
    ordered = []
    for member in range(4):
        held = received[0]
        for offset in range(1, 4):
            held = jnp.where(jnp.bitwise_xor(place, member) == offset, received[offset], held)
        ordered.append(held)
    return (ordered[0] + ordered[1]) + (ordered[2] + ordered[3])


def all_sum(value):
    shape = value.shape
    value = value.reshape(-1, 128)
    upper = lax.axis_index("blk") % 2
    half = value.shape[0] // 2
    low, high = value[:half], value[half:]
    keep = jnp.where(upper == 0, low, high)
    value = keep + swap(jnp.where(upper == 0, high, low), "blk", 1)
    value = group_sum(value, "blk", 2)
    value = group_sum(value, "blk", 8)
    value = group_sum(value, "row", 1)
    stride = 4
    while stride < lax.axis_size("row"):
        value = value + swap(value, "row", stride)
        stride *= 2
    other = swap(value, "blk", 1)
    value = jnp.where(upper == 0, jnp.concatenate([value, other]), jnp.concatenate([other, value]))
    return value.reshape(shape)


def per_device(samples, blocks, factor):
    width = BLOCK
    row_count = lax.axis_size("row")
    count = width // row_count
    row_lo = lax.axis_index("row") * count
    per_owner = blocks.shape[0] // lax.axis_size("blk")
    mine = lax.dynamic_slice_in_dim(blocks, lax.axis_index("blk") * per_owner, per_owner, 0)
    needed = mine.reshape(-1)
    pairs = width * width
    piece = jnp.concatenate([samples, swap(samples, "blk", 1)], axis=0)
    for stride in (2, 8):
        piece = jnp.concatenate([piece] + [swap(piece, "blk", stride * member) for member in range(1, 4)], axis=0)
    pieces = piece.shape[0] // width
    owned = jnp.bitwise_xor(lax.axis_index("blk"), jnp.arange(pieces, dtype=jnp.int32))
    select = (needed[:, None] == owned[None, :]).astype(jnp.bfloat16)
    shaped = piece.reshape(pieces, width, piece.shape[1])
    taken = jnp.einsum("mb,bcs->mcs", select, shaped, preferred_element_type=jnp.float32)
    local = taken.astype(jnp.bfloat16)
    forward = [(index, (index + 1) % row_count) for index in range(row_count)]
    backward = [(index, (index - 1) % row_count) for index in range(row_count)]
    piece_rows = 4 * width
    chunks = [local[4 * slot : 4 * slot + 4] for slot in range(per_owner)]
    moments = [jnp.zeros((count * width, pairs), jnp.float32) for _ in range(per_owner)]
    grams = [jnp.zeros((piece_rows, piece_rows), jnp.float32) for _ in range(per_owner)]
    held = factor
    held_pieces = []
    for step in range(row_count):
        if step + 1 < row_count:
            incoming = [
                lax.ppermute(chunks[slot], "row", forward if slot % 2 == 0 else backward)
                for slot in range(per_owner)
            ]
            held_in = lax.ppermute(held, "row", forward)
        held_pieces.append(held)
        for slot in range(per_owner):
            chunk = chunks[slot]
            left = lax.dynamic_slice_in_dim(chunk[0], row_lo, count, 0)
            moments[slot], grams[slot] = moment_step(left, chunk, moments[slot], grams[slot])
        if step + 1 < row_count:
            chunks, held = incoming, held_in
    slabs = []
    for slot in range(per_owner):
        moment = moments[slot] / SAMPLES
        gram = grams[slot] / SAMPLES
        slabs.append(cumulant_slab(moment, gram, count, width, row_lo))
    source = (lax.axis_index("row") - jnp.arange(row_count)) % row_count
    stacked = jnp.stack(held_pieces)[source]
    full = jnp.transpose(stacked, (1, 0, 2)).reshape(factor.shape[0], -1)
    for step in range(ITERS):
        grad = jnp.zeros(full.shape, jnp.float32)
        for slot in range(per_owner):
            grad = add_grads(grad, slabs[slot], full, mine[slot], row_lo, count, width)
        grad = all_sum(grad)
        scale = lax.rsqrt(jnp.mean(grad * grad) + 1e-06)
        full = full + step_size * scale * grad
    col_count = factor.shape[1]
    columns = lax.dynamic_slice_in_dim(full, lax.axis_index("row") * col_count, col_count, 1)
    return (jnp.stack(slabs), columns)


def solution(mesh):
    placed = (P("blk", "row"), P(), P(None, "row"))
    return jax.shard_map(
        per_device,
        mesh=mesh,
        in_specs=placed,
        out_specs=(P("blk", "row", None), P(None, "row")),
        check_vma=False,
    )
```

```python
import jax
import jax.numpy as jnp
from jax import lax
from jax.experimental import pallas as pl
from jax.experimental.pallas import tpu as pltpu
from jax.sharding import PartitionSpec as P

CHANNELS = 1024
BLOCK = 32
RANK = 64
SAMPLES = 8192
ITERS = 2


step_size = 0.2


def pair_rows(left, right):
    product = left[:, None, :].astype(jnp.float32) * right[None, :, :].astype(jnp.float32)
    return product.reshape(left.shape[0] * right.shape[0], left.shape[1]).astype(jnp.bfloat16)


def contract_last(left, right):
    return lax.dot_general(
        left, right, (((1,), (1,)), ((), ())), preferred_element_type=jnp.float32
    )


def spread(values, width, major):
    place = jnp.arange(width * width, dtype=jnp.int32)
    index = place // width if major else place % width
    pick = (index[None, :] == jnp.arange(width, dtype=jnp.int32)[:, None]).astype(values.dtype)
    return jnp.dot(values, pick, precision=lax.Precision.HIGHEST)


def cumulant_slab(moment, gram, count, width, row_lo):
    def part(first, second):
        return gram[first * width : (first + 1) * width, second * width : (second + 1) * width]

    cov_ab = lax.dynamic_slice_in_dim(part(0, 1), row_lo, count, 0)
    cov_ac = lax.dynamic_slice_in_dim(part(0, 2), row_lo, count, 0)
    cov_ad = lax.dynamic_slice_in_dim(part(0, 3), row_lo, count, 0)
    cov_cd = part(2, 3)
    cov_bd = part(1, 3)
    cov_bc = part(1, 2)
    first_term = cov_ab[:, :, None] * cov_cd.reshape(1, 1, width * width)
    second_term = spread(cov_ac, width, True)[:, None, :] * spread(cov_bd, width, False)[None, :, :]
    third_term = spread(cov_ad, width, False)[:, None, :] * spread(cov_bc, width, True)[None, :, :]
    shaped = moment.reshape(count, width, width * width)
    slab = shaped - ((first_term + second_term) + third_term)
    return slab.reshape(count * width, width * width)


def add_cols(total, piece, start):
    old = lax.dynamic_slice_in_dim(total, start, piece.shape[1], 1)
    return lax.dynamic_update_slice_in_dim(total, old + piece, start, 1)


def add_grads(total, kslab, full, ids, row_lo, count, width):
    highest = lax.Precision.HIGHEST
    rank = full.shape[0]
    start_a = ids[0] * width + row_lo
    fac_a = lax.dynamic_slice_in_dim(full, start_a, count, 1)
    fac_b = lax.dynamic_slice_in_dim(full, ids[1] * width, width, 1)
    fac_c = lax.dynamic_slice_in_dim(full, ids[2] * width, width, 1)
    fac_d = lax.dynamic_slice_in_dim(full, ids[3] * width, width, 1)
    upair = (fac_a[:, :, None] * fac_b[:, None, :]).reshape(rank, count * width)
    vpair = (fac_c[:, :, None] * fac_d[:, None, :]).reshape(rank, width * width)
    model = lax.dot_general(upair, vpair, (((0,), (0,)), ((), ())), precision=highest)
    resid = kslab - model
    wmat = lax.dot_general(vpair, resid, (((1,), (1,)), ((), ())), precision=highest).reshape(
        rank, count, width
    )
    zmat = jnp.dot(upair, resid, precision=highest).reshape(rank, width, width)
    total = add_cols(total, jnp.sum(wmat * fac_b[:, None, :], axis=2), start_a)
    total = add_cols(total, jnp.sum(wmat * fac_a[:, :, None], axis=1), ids[1] * width)
    total = add_cols(total, jnp.sum(zmat * fac_d[:, None, :], axis=2), ids[2] * width)
    total = add_cols(total, jnp.sum(zmat * fac_c[:, :, None], axis=1), ids[3] * width)
    return total


def moment_kernel(left_ref, chunk_ref, moment_ref, gram_ref, moment_out, gram_out, qmat_ref, pmat_ref):
    width = chunk_ref.shape[1]
    count = left_ref.shape[0]
    right = chunk_ref[1].astype(jnp.float32)
    for i in range(count):
        pmat_ref[pl.ds(i * width, width), :] = (left_ref[pl.ds(i, 1), :].astype(jnp.float32) * right).astype(jnp.bfloat16)
    fourth = chunk_ref[3].astype(jnp.float32)

    def build(group, carry):
        low = pl.multiple_of(group * 8, 8)
        thirds = chunk_ref[2, pl.ds(low, 8), :].astype(jnp.float32)
        for row in range(8):
            start = pl.multiple_of((low + row) * width, width)
            qmat_ref[pl.ds(start, width), :] = (thirds[row : row + 1, :] * fourth).astype(jnp.bfloat16)
        return carry

    lax.fori_loop(0, width // 8, build, 0)
    dims = (((1,), (1,)), ((), ()))
    moment_out[...] = moment_ref[...] + lax.dot_general(
        pmat_ref[...], qmat_ref[...], dims, preferred_element_type=jnp.float32)
    joined = chunk_ref[...].reshape(4 * width, chunk_ref.shape[2])
    gram_out[...] = gram_ref[...] + lax.dot_general(joined, joined, dims, preferred_element_type=jnp.float32)

def moment_step(left, chunk, moment, gram):
    width = chunk.shape[1]
    samples = chunk.shape[2]
    spec = pl.BlockSpec(memory_space=pltpu.MemorySpace.VMEM)
    return pl.pallas_call(
        moment_kernel,
        out_shape=(jax.ShapeDtypeStruct(moment.shape, jnp.float32), jax.ShapeDtypeStruct(gram.shape, jnp.float32)),
        in_specs=[spec] * 4,
        out_specs=(spec, spec),
        scratch_shapes=[pltpu.VMEM((width * width, samples), jnp.bfloat16),
                        pltpu.VMEM((left.shape[0] * width, samples), jnp.bfloat16)],
        input_output_aliases={2: 0, 3: 1},
        cost_estimate=pl.CostEstimate(
            flops=2 * moment.size * samples + 2 * gram.size * samples + 3 * width * width * samples,
            transcendentals=0,
            bytes_accessed=2 * (moment.size + gram.size) * 4 + chunk.size * 2 + left.size * 2,
        ),
    )(left, chunk, moment, gram)


def gather_factor(columns):
    stacked = lax.all_gather(columns, "row", axis=0)
    return jnp.transpose(stacked, (1, 0, 2)).reshape(columns.shape[0], -1)


def swap(value, axis, stride):
    size = lax.axis_size(axis)
    return lax.ppermute(value, axis, [(index, index ^ stride) for index in range(size)])


def group_sum(value, axis, stride):
    place = (lax.axis_index(axis) // stride) % 4
    received = [value] + [swap(value, axis, stride * member) for member in range(1, 4)]
    ordered = []
    for member in range(4):
        held = received[0]
        for offset in range(1, 4):
            held = jnp.where(jnp.bitwise_xor(place, member) == offset, received[offset], held)
        ordered.append(held)
    return (ordered[0] + ordered[1]) + (ordered[2] + ordered[3])


def all_sum(value):
    shape = value.shape
    value = value.reshape(-1, 128)
    upper = lax.axis_index("blk") % 2
    half = value.shape[0] // 2
    low, high = value[:half], value[half:]
    keep = jnp.where(upper == 0, low, high)
    value = keep + swap(jnp.where(upper == 0, high, low), "blk", 1)
    value = group_sum(value, "blk", 2)
    value = group_sum(value, "blk", 8)
    value = group_sum(value, "row", 1)
    stride = 4
    while stride < lax.axis_size("row"):
        value = value + swap(value, "row", stride)
        stride *= 2
    other = swap(value, "blk", 1)
    value = jnp.where(upper == 0, jnp.concatenate([value, other]), jnp.concatenate([other, value]))
    return value.reshape(shape)


def per_device(samples, blocks, factor):
    width = BLOCK
    row_count = lax.axis_size("row")
    count = width // row_count
    row_lo = lax.axis_index("row") * count
    per_owner = blocks.shape[0] // lax.axis_size("blk")
    mine = lax.dynamic_slice_in_dim(blocks, lax.axis_index("blk") * per_owner, per_owner, 0)
    needed = mine.reshape(-1)
    pairs = width * width
    piece = jnp.concatenate([samples, swap(samples, "blk", 1)], axis=0)
    for stride in (2, 8):
        piece = jnp.concatenate([piece] + [swap(piece, "blk", stride * member) for member in range(1, 4)], axis=0)
    pieces = piece.shape[0] // width
    owned = jnp.bitwise_xor(lax.axis_index("blk"), jnp.arange(pieces, dtype=jnp.int32))
    select = (needed[:, None] == owned[None, :]).astype(jnp.bfloat16)
    shaped = piece.reshape(pieces, width, piece.shape[1])
    taken = jnp.einsum("mb,bcs->mcs", select, shaped, preferred_element_type=jnp.float32)
    local = taken.astype(jnp.bfloat16)
    forward = [(index, (index + 1) % row_count) for index in range(row_count)]
    backward = [(index, (index - 1) % row_count) for index in range(row_count)]
    piece_rows = 4 * width
    chunks = [local[4 * slot : 4 * slot + 4] for slot in range(per_owner)]
    moments = [jnp.zeros((count * width, pairs), jnp.float32) for _ in range(per_owner)]
    grams = [jnp.zeros((piece_rows, piece_rows), jnp.float32) for _ in range(per_owner)]
    for step in range(row_count):
        if step + 1 < row_count:
            incoming = [
                lax.ppermute(chunks[slot], "row", forward if slot % 2 == 0 else backward)
                for slot in range(per_owner)
            ]
        for slot in range(per_owner):
            chunk = chunks[slot]
            left = lax.dynamic_slice_in_dim(chunk[0], row_lo, count, 0)
            moments[slot], grams[slot] = moment_step(left, chunk, moments[slot], grams[slot])
        if step + 1 < row_count:
            chunks = incoming
    slabs = []
    for slot in range(per_owner):
        moment = moments[slot] / SAMPLES
        gram = grams[slot] / SAMPLES
        slabs.append(cumulant_slab(moment, gram, count, width, row_lo))
    held = factor[None]
    held = jnp.concatenate([held] + [swap(held, "row", member) for member in range(1, 4)], axis=0)
    held = jnp.concatenate([held, swap(held, "row", 4)], axis=0)
    source = jnp.bitwise_xor(lax.axis_index("row"), jnp.arange(row_count, dtype=jnp.int32))
    stacked = held[source]
    full = jnp.transpose(stacked, (1, 0, 2)).reshape(factor.shape[0], -1)
    for step in range(ITERS):
        grad = jnp.zeros(full.shape, jnp.float32)
        for slot in range(per_owner):
            grad = add_grads(grad, slabs[slot], full, mine[slot], row_lo, count, width)
        grad = all_sum(grad)
        scale = lax.rsqrt(jnp.mean(grad * grad) + 1e-06)
        full = full + step_size * scale * grad
    col_count = factor.shape[1]
    columns = lax.dynamic_slice_in_dim(full, lax.axis_index("row") * col_count, col_count, 1)
    return (jnp.stack(slabs), columns)


def solution(mesh):
    placed = (P("blk", "row"), P(), P(None, "row"))
    return jax.shard_map(
        per_device,
        mesh=mesh,
        in_specs=placed,
        out_specs=(P("blk", "row", None), P(None, "row")),
        check_vma=False,
    )
```

```python
import jax
import jax.numpy as jnp
from jax import lax
from jax.experimental import pallas as pl
from jax.experimental.pallas import tpu as pltpu
from jax.sharding import PartitionSpec as P

CHANNELS = 1024
BLOCK = 32
RANK = 64
SAMPLES = 8192
ITERS = 2


step_size = 0.2


def pair_rows(left, right):
    product = left[:, None, :].astype(jnp.float32) * right[None, :, :].astype(jnp.float32)
    return product.reshape(left.shape[0] * right.shape[0], left.shape[1]).astype(jnp.bfloat16)


def contract_last(left, right):
    return lax.dot_general(
        left, right, (((1,), (1,)), ((), ())), preferred_element_type=jnp.float32
    )


def spread(values, width, major):
    place = jnp.arange(width * width, dtype=jnp.int32)
    index = place // width if major else place % width
    pick = (index[None, :] == jnp.arange(width, dtype=jnp.int32)[:, None]).astype(values.dtype)
    return jnp.dot(values, pick, precision=lax.Precision.HIGHEST)


def cumulant_slab(moment, gram, count, width, row_lo):
    def part(first, second):
        return gram[first * width : (first + 1) * width, second * width : (second + 1) * width]

    cov_ab = lax.dynamic_slice_in_dim(part(0, 1), row_lo, count, 0)
    cov_ac = lax.dynamic_slice_in_dim(part(0, 2), row_lo, count, 0)
    cov_ad = lax.dynamic_slice_in_dim(part(0, 3), row_lo, count, 0)
    cov_cd = part(2, 3)
    cov_bd = part(1, 3)
    cov_bc = part(1, 2)
    first_term = cov_ab[:, :, None] * cov_cd.reshape(1, 1, width * width)
    second_term = spread(cov_ac, width, True)[:, None, :] * spread(cov_bd, width, False)[None, :, :]
    third_term = spread(cov_ad, width, False)[:, None, :] * spread(cov_bc, width, True)[None, :, :]
    shaped = moment.reshape(count, width, width * width)
    slab = shaped - ((first_term + second_term) + third_term)
    return slab.reshape(count * width, width * width)


def add_cols(total, piece, start):
    old = lax.dynamic_slice_in_dim(total, start, piece.shape[1], 1)
    return lax.dynamic_update_slice_in_dim(total, old + piece, start, 1)


def add_grads(total, kslab, full, ids, row_lo, count, width):
    highest = lax.Precision.HIGHEST
    rank = full.shape[0]
    start_a = ids[0] * width + row_lo
    fac_a = lax.dynamic_slice_in_dim(full, start_a, count, 1)
    fac_b = lax.dynamic_slice_in_dim(full, ids[1] * width, width, 1)
    fac_c = lax.dynamic_slice_in_dim(full, ids[2] * width, width, 1)
    fac_d = lax.dynamic_slice_in_dim(full, ids[3] * width, width, 1)
    upair = (fac_a[:, :, None] * fac_b[:, None, :]).reshape(rank, count * width)
    vpair = (fac_c[:, :, None] * fac_d[:, None, :]).reshape(rank, width * width)
    model = lax.dot_general(upair, vpair, (((0,), (0,)), ((), ())), precision=highest)
    resid = kslab - model
    wmat = lax.dot_general(vpair, resid, (((1,), (1,)), ((), ())), precision=highest).reshape(
        rank, count, width
    )
    zmat = jnp.dot(upair, resid, precision=highest).reshape(rank, width, width)
    total = add_cols(total, jnp.sum(wmat * fac_b[:, None, :], axis=2), start_a)
    total = add_cols(total, jnp.sum(wmat * fac_a[:, :, None], axis=1), ids[1] * width)
    total = add_cols(total, jnp.sum(zmat * fac_d[:, None, :], axis=2), ids[2] * width)
    total = add_cols(total, jnp.sum(zmat * fac_c[:, :, None], axis=1), ids[3] * width)
    return total


def moment_kernel(*refs):
    slots = (len(refs) - 2) // 6
    lefts, chunks, moments, grams = (refs[index * slots : (index + 1) * slots] for index in range(4))
    moment_outs = refs[4 * slots : 5 * slots]
    gram_outs = refs[5 * slots : 6 * slots]
    qmat_ref, pmat_ref = refs[6 * slots :]
    for slot in range(slots):
        left_ref, chunk_ref = lefts[slot], chunks[slot]
        width = chunk_ref.shape[1]
        count = left_ref.shape[0]
        right = chunk_ref[1].astype(jnp.float32)
        for i in range(count):
            pmat_ref[pl.ds(i * width, width), :] = (left_ref[pl.ds(i, 1), :].astype(jnp.float32) * right).astype(
                jnp.bfloat16
            )
        fourth = chunk_ref[3].astype(jnp.float32)

        def build(group, carry, chunk_ref=chunk_ref, fourth=fourth, width=width):
            low = pl.multiple_of(group * 8, 8)
            thirds = chunk_ref[2, pl.ds(low, 8), :].astype(jnp.float32)
            for row in range(8):
                start = pl.multiple_of((low + row) * width, width)
                qmat_ref[pl.ds(start, width), :] = (thirds[row : row + 1, :] * fourth).astype(jnp.bfloat16)
            return carry

        lax.fori_loop(0, width // 8, build, 0)
        dims = (((1,), (1,)), ((), ()))
        moment_outs[slot][...] = moments[slot][...] + lax.dot_general(
            pmat_ref[...], qmat_ref[...], dims, preferred_element_type=jnp.float32
        )
        joined = chunk_ref[...].reshape(4 * width, chunk_ref.shape[2])
        gram_outs[slot][...] = grams[slot][...] + lax.dot_general(
            joined, joined, dims, preferred_element_type=jnp.float32
        )


def moment_step(lefts, chunks, moments, grams):
    slots = len(chunks)
    width = chunks[0].shape[1]
    samples = chunks[0].shape[2]
    spec = pl.BlockSpec(memory_space=pltpu.MemorySpace.VMEM)
    shapes = [jax.ShapeDtypeStruct(m.shape, jnp.float32) for m in moments]
    shapes += [jax.ShapeDtypeStruct(g.shape, jnp.float32) for g in grams]
    per_slot_flops = 2 * moments[0].size * samples + 2 * grams[0].size * samples + 3 * width * width * samples
    per_slot_bytes = 2 * (moments[0].size + grams[0].size) * 4 + chunks[0].size * 2 + lefts[0].size * 2
    outs = pl.pallas_call(
        moment_kernel,
        out_shape=tuple(shapes),
        in_specs=[spec] * (4 * slots),
        out_specs=tuple([spec] * (2 * slots)),
        scratch_shapes=[
            pltpu.VMEM((width * width, samples), jnp.bfloat16),
            pltpu.VMEM((lefts[0].shape[0] * width, samples), jnp.bfloat16),
        ],
        input_output_aliases={2 * slots + index: index for index in range(2 * slots)},
        cost_estimate=pl.CostEstimate(
            flops=slots * per_slot_flops, transcendentals=0, bytes_accessed=slots * per_slot_bytes
        ),
    )(*lefts, *chunks, *moments, *grams)
    return list(outs[:slots]), list(outs[slots:])


def gather_factor(columns):
    stacked = lax.all_gather(columns, "row", axis=0)
    return jnp.transpose(stacked, (1, 0, 2)).reshape(columns.shape[0], -1)


def swap(value, axis, stride):
    size = lax.axis_size(axis)
    return lax.ppermute(value, axis, [(index, index ^ stride) for index in range(size)])


def group_sum(value, axis, stride):
    place = (lax.axis_index(axis) // stride) % 4
    received = [value] + [swap(value, axis, stride * member) for member in range(1, 4)]
    ordered = []
    for member in range(4):
        held = received[0]
        for offset in range(1, 4):
            held = jnp.where(jnp.bitwise_xor(place, member) == offset, received[offset], held)
        ordered.append(held)
    return (ordered[0] + ordered[1]) + (ordered[2] + ordered[3])


def all_sum(value):
    shape = value.shape
    value = value.reshape(-1, 128)
    upper = lax.axis_index("blk") % 2
    half = value.shape[0] // 2
    low, high = value[:half], value[half:]
    keep = jnp.where(upper == 0, low, high)
    value = keep + swap(jnp.where(upper == 0, high, low), "blk", 1)
    value = group_sum(value, "blk", 2)
    value = group_sum(value, "blk", 8)
    value = group_sum(value, "row", 1)
    stride = 4
    while stride < lax.axis_size("row"):
        value = value + swap(value, "row", stride)
        stride *= 2
    other = swap(value, "blk", 1)
    value = jnp.where(upper == 0, jnp.concatenate([value, other]), jnp.concatenate([other, value]))
    return value.reshape(shape)


def per_device(samples, blocks, factor):
    width = BLOCK
    row_count = lax.axis_size("row")
    count = width // row_count
    row_lo = lax.axis_index("row") * count
    per_owner = blocks.shape[0] // lax.axis_size("blk")
    mine = lax.dynamic_slice_in_dim(blocks, lax.axis_index("blk") * per_owner, per_owner, 0)
    needed = mine.reshape(-1)
    pairs = width * width
    piece = jnp.concatenate([samples, swap(samples, "blk", 1)], axis=0)
    for stride in (2, 8):
        piece = jnp.concatenate([piece] + [swap(piece, "blk", stride * member) for member in range(1, 4)], axis=0)
    pieces = piece.shape[0] // width
    owned = jnp.bitwise_xor(lax.axis_index("blk"), jnp.arange(pieces, dtype=jnp.int32))
    select = (needed[:, None] == owned[None, :]).astype(jnp.bfloat16)
    shaped = piece.reshape(pieces, width, piece.shape[1])
    taken = jnp.einsum("mb,bcs->mcs", select, shaped, preferred_element_type=jnp.float32)
    local = taken.astype(jnp.bfloat16)
    forward = [(index, (index + 1) % row_count) for index in range(row_count)]
    backward = [(index, (index - 1) % row_count) for index in range(row_count)]
    piece_rows = 4 * width
    chunks = [local[4 * slot : 4 * slot + 4] for slot in range(per_owner)]
    moments = [jnp.zeros((count * width, pairs), jnp.float32) for _ in range(per_owner)]
    grams = [jnp.zeros((piece_rows, piece_rows), jnp.float32) for _ in range(per_owner)]
    held = factor
    held_pieces = []
    for step in range(row_count):
        if step + 1 < row_count:
            incoming = [
                lax.ppermute(chunks[slot], "row", forward if slot % 2 == 0 else backward)
                for slot in range(per_owner)
            ]
            held_in = lax.ppermute(held, "row", forward)
        held_pieces.append(held)
        lefts = [lax.dynamic_slice_in_dim(chunk[0], row_lo, count, 0) for chunk in chunks]
        moments, grams = moment_step(lefts, chunks, moments, grams)
        if step + 1 < row_count:
            chunks, held = incoming, held_in
    slabs = []
    for slot in range(per_owner):
        moment = moments[slot] / SAMPLES
        gram = grams[slot] / SAMPLES
        slabs.append(cumulant_slab(moment, gram, count, width, row_lo))
    source = (lax.axis_index("row") - jnp.arange(row_count)) % row_count
    stacked = jnp.stack(held_pieces)[source]
    full = jnp.transpose(stacked, (1, 0, 2)).reshape(factor.shape[0], -1)
    for step in range(ITERS):
        grad = jnp.zeros(full.shape, jnp.float32)
        for slot in range(per_owner):
            grad = add_grads(grad, slabs[slot], full, mine[slot], row_lo, count, width)
        grad = all_sum(grad)
        scale = lax.rsqrt(jnp.mean(grad * grad) + 1e-06)
        full = full + step_size * scale * grad
    col_count = factor.shape[1]
    columns = lax.dynamic_slice_in_dim(full, lax.axis_index("row") * col_count, col_count, 1)
    return (jnp.stack(slabs), columns)


def solution(mesh):
    placed = (P("blk", "row"), P(), P(None, "row"))
    return jax.shard_map(
        per_device,
        mesh=mesh,
        in_specs=placed,
        out_specs=(P("blk", "row", None), P(None, "row")),
        check_vma=False,
    )
```

```python
import jax
import jax.numpy as jnp
from jax import lax
from jax.experimental import pallas as pl
from jax.experimental.pallas import tpu as pltpu
from jax.sharding import PartitionSpec as P

CHANNELS = 1024
BLOCK = 32
RANK = 64
SAMPLES = 8192
ITERS = 2


step_size = 0.2


def pair_rows(left, right):
    product = left[:, None, :].astype(jnp.float32) * right[None, :, :].astype(jnp.float32)
    return product.reshape(left.shape[0] * right.shape[0], left.shape[1]).astype(jnp.bfloat16)


def contract_last(left, right):
    return lax.dot_general(
        left, right, (((1,), (1,)), ((), ())), preferred_element_type=jnp.float32
    )


def spread(values, width, major):
    place = jnp.arange(width * width, dtype=jnp.int32)
    index = place // width if major else place % width
    pick = (index[None, :] == jnp.arange(width, dtype=jnp.int32)[:, None]).astype(values.dtype)
    return jnp.dot(values, pick, precision=lax.Precision.HIGHEST)


def cumulant_slab(moment, gram, count, width, row_lo):
    def part(first, second):
        return gram[first * width : (first + 1) * width, second * width : (second + 1) * width]

    cov_ab = lax.dynamic_slice_in_dim(part(0, 1), row_lo, count, 0)
    cov_ac = lax.dynamic_slice_in_dim(part(0, 2), row_lo, count, 0)
    cov_ad = lax.dynamic_slice_in_dim(part(0, 3), row_lo, count, 0)
    cov_cd = part(2, 3)
    cov_bd = part(1, 3)
    cov_bc = part(1, 2)
    first_term = cov_ab[:, :, None] * cov_cd.reshape(1, 1, width * width)
    second_term = spread(cov_ac, width, True)[:, None, :] * spread(cov_bd, width, False)[None, :, :]
    third_term = spread(cov_ad, width, False)[:, None, :] * spread(cov_bc, width, True)[None, :, :]
    shaped = moment.reshape(count, width, width * width)
    slab = shaped - ((first_term + second_term) + third_term)
    return slab.reshape(count * width, width * width)


def add_cols(total, piece, start):
    old = lax.dynamic_slice_in_dim(total, start, piece.shape[1], 1)
    return lax.dynamic_update_slice_in_dim(total, old + piece, start, 1)


def add_grads(total, kslab, full, ids, row_lo, count, width):
    highest = lax.Precision.HIGHEST
    rank = full.shape[0]
    start_a = ids[0] * width + row_lo
    fac_a = lax.dynamic_slice_in_dim(full, start_a, count, 1)
    fac_b = lax.dynamic_slice_in_dim(full, ids[1] * width, width, 1)
    fac_c = lax.dynamic_slice_in_dim(full, ids[2] * width, width, 1)
    fac_d = lax.dynamic_slice_in_dim(full, ids[3] * width, width, 1)
    upair = (fac_a[:, :, None] * fac_b[:, None, :]).reshape(rank, count * width)
    vpair = (fac_c[:, :, None] * fac_d[:, None, :]).reshape(rank, width * width)
    model = lax.dot_general(upair, vpair, (((0,), (0,)), ((), ())), precision=highest)
    resid = kslab - model
    wmat = lax.dot_general(vpair, resid, (((1,), (1,)), ((), ())), precision=highest).reshape(
        rank, count, width
    )
    zmat = jnp.dot(upair, resid, precision=highest).reshape(rank, width, width)
    total = add_cols(total, jnp.sum(wmat * fac_b[:, None, :], axis=2), start_a)
    total = add_cols(total, jnp.sum(wmat * fac_a[:, :, None], axis=1), ids[1] * width)
    total = add_cols(total, jnp.sum(zmat * fac_d[:, None, :], axis=2), ids[2] * width)
    total = add_cols(total, jnp.sum(zmat * fac_c[:, :, None], axis=1), ids[3] * width)
    return total


def moment_kernel(*refs):
    slots = (len(refs) - 2) // 6
    lefts, chunks, moments, grams = (refs[index * slots : (index + 1) * slots] for index in range(4))
    moment_outs = refs[4 * slots : 5 * slots]
    gram_outs = refs[5 * slots : 6 * slots]
    qmat_ref, pmat_ref = refs[6 * slots :]
    for slot in range(slots):
        left_ref, chunk_ref = lefts[slot], chunks[slot]
        width = chunk_ref.shape[1]
        count = left_ref.shape[0]
        right = chunk_ref[1].astype(jnp.float32)
        for i in range(count):
            pmat_ref[pl.ds(i * width, width), :] = (left_ref[pl.ds(i, 1), :].astype(jnp.float32) * right).astype(
                jnp.bfloat16
            )
        fourth = chunk_ref[3].astype(jnp.float32)

        def build(group, carry, chunk_ref=chunk_ref, fourth=fourth, width=width):
            low = pl.multiple_of(group * 8, 8)
            thirds = chunk_ref[2, pl.ds(low, 8), :].astype(jnp.float32)
            for row in range(8):
                start = pl.multiple_of((low + row) * width, width)
                qmat_ref[pl.ds(start, width), :] = (thirds[row : row + 1, :] * fourth).astype(jnp.bfloat16)
            return carry

        lax.fori_loop(0, width // 8, build, 0)
        dims = (((1,), (1,)), ((), ()))
        moment_outs[slot][...] = moments[slot][...] + lax.dot_general(
            pmat_ref[...], qmat_ref[...], dims, preferred_element_type=jnp.float32
        )
        joined = chunk_ref[...].reshape(4 * width, chunk_ref.shape[2])
        gram_outs[slot][...] = grams[slot][...] + lax.dot_general(
            joined, joined, dims, preferred_element_type=jnp.float32
        )


def moment_step(lefts, chunks, moments, grams):
    slots = len(chunks)
    width = chunks[0].shape[1]
    samples = chunks[0].shape[2]
    spec = pl.BlockSpec(memory_space=pltpu.MemorySpace.VMEM)
    shapes = [jax.ShapeDtypeStruct(m.shape, jnp.float32) for m in moments]
    shapes += [jax.ShapeDtypeStruct(g.shape, jnp.float32) for g in grams]
    per_slot_flops = 2 * moments[0].size * samples + 2 * grams[0].size * samples + 3 * width * width * samples
    per_slot_bytes = 2 * (moments[0].size + grams[0].size) * 4 + chunks[0].size * 2 + lefts[0].size * 2
    outs = pl.pallas_call(
        moment_kernel,
        out_shape=tuple(shapes),
        in_specs=[spec] * (4 * slots),
        out_specs=tuple([spec] * (2 * slots)),
        scratch_shapes=[
            pltpu.VMEM((width * width, samples), jnp.bfloat16),
            pltpu.VMEM((lefts[0].shape[0] * width, samples), jnp.bfloat16),
        ],
        input_output_aliases={2 * slots + index: index for index in range(2 * slots)},
        cost_estimate=pl.CostEstimate(
            flops=slots * per_slot_flops, transcendentals=0, bytes_accessed=slots * per_slot_bytes
        ),
    )(*lefts, *chunks, *moments, *grams)
    return list(outs[:slots]), list(outs[slots:])


def gather_factor(columns):
    stacked = lax.all_gather(columns, "row", axis=0)
    return jnp.transpose(stacked, (1, 0, 2)).reshape(columns.shape[0], -1)


def swap(value, axis, stride):
    size = lax.axis_size(axis)
    return lax.ppermute(value, axis, [(index, index ^ stride) for index in range(size)])


def group_sum(value, axis, stride):
    place = (lax.axis_index(axis) // stride) % 4
    received = [value] + [swap(value, axis, stride * member) for member in range(1, 4)]
    ordered = []
    for member in range(4):
        held = received[0]
        for offset in range(1, 4):
            held = jnp.where(jnp.bitwise_xor(place, member) == offset, received[offset], held)
        ordered.append(held)
    return (ordered[0] + ordered[1]) + (ordered[2] + ordered[3])


def all_sum(value):
    shape = value.shape
    value = value.reshape(-1, 128)
    upper = lax.axis_index("blk") % 2
    half = value.shape[0] // 2
    low, high = value[:half], value[half:]
    keep = jnp.where(upper == 0, low, high)
    value = keep + swap(jnp.where(upper == 0, high, low), "blk", 1)
    value = group_sum(value, "blk", 2)
    value = group_sum(value, "blk", 8)
    value = group_sum(value, "row", 1)
    stride = 4
    while stride < lax.axis_size("row"):
        value = value + swap(value, "row", stride)
        stride *= 2
    other = swap(value, "blk", 1)
    value = jnp.where(upper == 0, jnp.concatenate([value, other]), jnp.concatenate([other, value]))
    return value.reshape(shape)


def per_device(samples, blocks, factor):
    width = BLOCK
    row_count = lax.axis_size("row")
    count = width // row_count
    row_lo = lax.axis_index("row") * count
    per_owner = blocks.shape[0] // lax.axis_size("blk")
    mine = lax.dynamic_slice_in_dim(blocks, lax.axis_index("blk") * per_owner, per_owner, 0)
    needed = mine.reshape(-1)
    pairs = width * width
    piece = samples
    for stride in (8, 2):
        piece = jnp.concatenate([piece] + [swap(piece, "blk", stride * member) for member in range(1, 4)], axis=0)
    piece = jnp.concatenate([piece, swap(piece, "blk", 1)], axis=0)
    pieces = piece.shape[0] // width
    offsets = [core + 2 * along_y + 8 * along_x for core in range(2) for along_y in range(4) for along_x in range(4)]
    owned = jnp.bitwise_xor(lax.axis_index("blk"), jnp.asarray(offsets, dtype=jnp.int32))
    select = (needed[:, None] == owned[None, :]).astype(jnp.bfloat16)
    shaped = piece.reshape(pieces, width, piece.shape[1])
    taken = jnp.einsum("mb,bcs->mcs", select, shaped, preferred_element_type=jnp.float32)
    local = taken.astype(jnp.bfloat16)
    forward = [(index, (index + 1) % row_count) for index in range(row_count)]
    backward = [(index, (index - 1) % row_count) for index in range(row_count)]
    piece_rows = 4 * width
    chunks = [local[4 * slot : 4 * slot + 4] for slot in range(per_owner)]
    moments = [jnp.zeros((count * width, pairs), jnp.float32) for _ in range(per_owner)]
    grams = [jnp.zeros((piece_rows, piece_rows), jnp.float32) for _ in range(per_owner)]
    held = factor
    held_pieces = []
    for step in range(row_count):
        if step + 1 < row_count:
            incoming = [
                lax.ppermute(chunks[slot], "row", forward if slot % 2 == 0 else backward)
                for slot in range(per_owner)
            ]
            held_in = lax.ppermute(held, "row", forward)
        held_pieces.append(held)
        lefts = [lax.dynamic_slice_in_dim(chunk[0], row_lo, count, 0) for chunk in chunks]
        moments, grams = moment_step(lefts, chunks, moments, grams)
        if step + 1 < row_count:
            chunks, held = incoming, held_in
    slabs = []
    for slot in range(per_owner):
        moment = moments[slot] / SAMPLES
        gram = grams[slot] / SAMPLES
        slabs.append(cumulant_slab(moment, gram, count, width, row_lo))
    source = (lax.axis_index("row") - jnp.arange(row_count)) % row_count
    stacked = jnp.stack(held_pieces)[source]
    full = jnp.transpose(stacked, (1, 0, 2)).reshape(factor.shape[0], -1)
    for step in range(ITERS):
        grad = jnp.zeros(full.shape, jnp.float32)
        for slot in range(per_owner):
            grad = add_grads(grad, slabs[slot], full, mine[slot], row_lo, count, width)
        grad = all_sum(grad)
        scale = lax.rsqrt(jnp.mean(grad * grad) + 1e-06)
        full = full + step_size * scale * grad
    col_count = factor.shape[1]
    columns = lax.dynamic_slice_in_dim(full, lax.axis_index("row") * col_count, col_count, 1)
    return (jnp.stack(slabs), columns)


def solution(mesh):
    placed = (P("blk", "row"), P(), P(None, "row"))
    return jax.shard_map(
        per_device,
        mesh=mesh,
        in_specs=placed,
        out_specs=(P("blk", "row", None), P(None, "row")),
        check_vma=False,
    )
```

```python
import jax
import jax.numpy as jnp
from jax import lax
from jax.experimental import pallas as pl
from jax.experimental.pallas import tpu as pltpu
from jax.sharding import PartitionSpec as P

CHANNELS = 1024
BLOCK = 32
RANK = 64
SAMPLES = 8192
ITERS = 2


step_size = 0.2


def pair_rows(left, right):
    product = left[:, None, :].astype(jnp.float32) * right[None, :, :].astype(jnp.float32)
    return product.reshape(left.shape[0] * right.shape[0], left.shape[1]).astype(jnp.bfloat16)


def contract_last(left, right):
    return lax.dot_general(
        left, right, (((1,), (1,)), ((), ())), preferred_element_type=jnp.float32
    )


def spread(values, width, major):
    place = jnp.arange(width * width, dtype=jnp.int32)
    index = place // width if major else place % width
    pick = (index[None, :] == jnp.arange(width, dtype=jnp.int32)[:, None]).astype(values.dtype)
    return jnp.dot(values, pick, precision=lax.Precision.HIGHEST)


def cumulant_slab(moment, gram, count, width, row_lo):
    def part(first, second):
        return gram[first * width : (first + 1) * width, second * width : (second + 1) * width]

    cov_ab = lax.dynamic_slice_in_dim(part(0, 1), row_lo, count, 0)
    cov_ac = lax.dynamic_slice_in_dim(part(0, 2), row_lo, count, 0)
    cov_ad = lax.dynamic_slice_in_dim(part(0, 3), row_lo, count, 0)
    cov_cd = part(2, 3)
    cov_bd = part(1, 3)
    cov_bc = part(1, 2)
    first_term = cov_ab[:, :, None] * cov_cd.reshape(1, 1, width * width)
    second_term = spread(cov_ac, width, True)[:, None, :] * spread(cov_bd, width, False)[None, :, :]
    third_term = spread(cov_ad, width, False)[:, None, :] * spread(cov_bc, width, True)[None, :, :]
    shaped = moment.reshape(count, width, width * width)
    slab = shaped - ((first_term + second_term) + third_term)
    return slab.reshape(count * width, width * width)


def add_cols(total, piece, start):
    old = lax.dynamic_slice_in_dim(total, start, piece.shape[1], 1)
    return lax.dynamic_update_slice_in_dim(total, old + piece, start, 1)


def add_grads(total, kslab, full, ids, row_lo, count, width):
    highest = lax.Precision.HIGHEST
    rank = full.shape[0]
    start_a = ids[0] * width + row_lo
    fac_a = lax.dynamic_slice_in_dim(full, start_a, count, 1)
    fac_b = lax.dynamic_slice_in_dim(full, ids[1] * width, width, 1)
    fac_c = lax.dynamic_slice_in_dim(full, ids[2] * width, width, 1)
    fac_d = lax.dynamic_slice_in_dim(full, ids[3] * width, width, 1)
    upair = (fac_a[:, :, None] * fac_b[:, None, :]).reshape(rank, count * width)
    vpair = (fac_c[:, :, None] * fac_d[:, None, :]).reshape(rank, width * width)
    model = lax.dot_general(upair, vpair, (((0,), (0,)), ((), ())), precision=highest)
    resid = kslab - model
    wmat = lax.dot_general(vpair, resid, (((1,), (1,)), ((), ())), precision=highest).reshape(
        rank, count, width
    )
    zmat = jnp.dot(upair, resid, precision=highest).reshape(rank, width, width)
    total = add_cols(total, jnp.sum(wmat * fac_b[:, None, :], axis=2), start_a)
    total = add_cols(total, jnp.sum(wmat * fac_a[:, :, None], axis=1), ids[1] * width)
    total = add_cols(total, jnp.sum(zmat * fac_d[:, None, :], axis=2), ids[2] * width)
    total = add_cols(total, jnp.sum(zmat * fac_c[:, :, None], axis=1), ids[3] * width)
    return total


def moment_kernel(*refs):
    slots = (len(refs) - 2) // 6
    lefts, chunks, moments, grams = (refs[index * slots : (index + 1) * slots] for index in range(4))
    moment_outs = refs[4 * slots : 5 * slots]
    gram_outs = refs[5 * slots : 6 * slots]
    qmat_ref, pmat_ref = refs[6 * slots :]
    for slot in range(slots):
        left_ref, chunk_ref = lefts[slot], chunks[slot]
        width = chunk_ref.shape[1]
        count = left_ref.shape[0]
        right = chunk_ref[1].astype(jnp.float32)
        left = lax.dot_general(
            left_ref[...], chunk_ref[0], (((1,), (0,)), ((), ())), preferred_element_type=jnp.float32
        )
        for i in range(count):
            pmat_ref[pl.ds(i * width, width), :] = (left[i : i + 1, :] * right).astype(jnp.bfloat16)
        fourth = chunk_ref[3].astype(jnp.float32)

        def build(group, carry, chunk_ref=chunk_ref, fourth=fourth, width=width):
            low = pl.multiple_of(group * 8, 8)
            thirds = chunk_ref[2, pl.ds(low, 8), :].astype(jnp.float32)
            for row in range(8):
                start = pl.multiple_of((low + row) * width, width)
                qmat_ref[pl.ds(start, width), :] = (thirds[row : row + 1, :] * fourth).astype(jnp.bfloat16)
            return carry

        lax.fori_loop(0, width // 8, build, 0)
        dims = (((1,), (1,)), ((), ()))
        moment_outs[slot][...] = moments[slot][...] + lax.dot_general(
            pmat_ref[...], qmat_ref[...], dims, preferred_element_type=jnp.float32
        )
        joined = chunk_ref[...].reshape(4 * width, chunk_ref.shape[2])
        gram_outs[slot][...] = grams[slot][...] + lax.dot_general(
            joined, joined, dims, preferred_element_type=jnp.float32
        )


def moment_step(lefts, chunks, moments, grams):
    slots = len(chunks)
    width = chunks[0].shape[1]
    samples = chunks[0].shape[2]
    spec = pl.BlockSpec(memory_space=pltpu.MemorySpace.VMEM)
    shapes = [jax.ShapeDtypeStruct(m.shape, jnp.float32) for m in moments]
    shapes += [jax.ShapeDtypeStruct(g.shape, jnp.float32) for g in grams]
    per_slot_flops = 2 * moments[0].size * samples + 2 * grams[0].size * samples + 3 * width * width * samples
    per_slot_bytes = 2 * (moments[0].size + grams[0].size) * 4 + chunks[0].size * 2 + lefts[0].size * 2
    outs = pl.pallas_call(
        moment_kernel,
        out_shape=tuple(shapes),
        in_specs=[spec] * (4 * slots),
        out_specs=tuple([spec] * (2 * slots)),
        scratch_shapes=[
            pltpu.VMEM((width * width, samples), jnp.bfloat16),
            pltpu.VMEM((lefts[0].shape[0] * width, samples), jnp.bfloat16),
        ],
        input_output_aliases={2 * slots + index: index for index in range(2 * slots)},
        cost_estimate=pl.CostEstimate(
            flops=slots * per_slot_flops, transcendentals=0, bytes_accessed=slots * per_slot_bytes
        ),
    )(*lefts, *chunks, *moments, *grams)
    return list(outs[:slots]), list(outs[slots:])


def gather_factor(columns):
    stacked = lax.all_gather(columns, "row", axis=0)
    return jnp.transpose(stacked, (1, 0, 2)).reshape(columns.shape[0], -1)


def swap(value, axis, stride):
    size = lax.axis_size(axis)
    return lax.ppermute(value, axis, [(index, index ^ stride) for index in range(size)])


def group_sum(value, axis, stride):
    place = (lax.axis_index(axis) // stride) % 4
    received = [value] + [swap(value, axis, stride * member) for member in range(1, 4)]
    ordered = []
    for member in range(4):
        held = received[0]
        for offset in range(1, 4):
            held = jnp.where(jnp.bitwise_xor(place, member) == offset, received[offset], held)
        ordered.append(held)
    return (ordered[0] + ordered[1]) + (ordered[2] + ordered[3])


def all_sum(value):
    shape = value.shape
    value = value.reshape(-1, 128)
    upper = lax.axis_index("blk") % 2
    half = value.shape[0] // 2
    low, high = value[:half], value[half:]
    keep = jnp.where(upper == 0, low, high)
    value = keep + swap(jnp.where(upper == 0, high, low), "blk", 1)
    value = group_sum(value, "blk", 2)
    value = group_sum(value, "blk", 8)
    value = group_sum(value, "row", 1)
    stride = 4
    while stride < lax.axis_size("row"):
        value = value + swap(value, "row", stride)
        stride *= 2
    other = swap(value, "blk", 1)
    value = jnp.where(upper == 0, jnp.concatenate([value, other]), jnp.concatenate([other, value]))
    return value.reshape(shape)


def per_device(samples, blocks, factor):
    width = BLOCK
    row_count = lax.axis_size("row")
    count = width // row_count
    row_lo = lax.axis_index("row") * count
    per_owner = blocks.shape[0] // lax.axis_size("blk")
    mine = lax.dynamic_slice_in_dim(blocks, lax.axis_index("blk") * per_owner, per_owner, 0)
    needed = mine.reshape(-1)
    pairs = width * width
    piece = jnp.concatenate([samples, swap(samples, "blk", 1)], axis=0)
    for stride in (2, 8):
        piece = jnp.concatenate([piece] + [swap(piece, "blk", stride * member) for member in range(1, 4)], axis=0)
    pieces = piece.shape[0] // width
    owned = jnp.bitwise_xor(lax.axis_index("blk"), jnp.arange(pieces, dtype=jnp.int32))
    select = (needed[:, None] == owned[None, :]).astype(jnp.bfloat16)
    shaped = piece.reshape(pieces, width, piece.shape[1])
    taken = jnp.einsum("mb,bcs->mcs", select, shaped, preferred_element_type=jnp.float32)
    local = taken.astype(jnp.bfloat16)
    forward = [(index, (index + 1) % row_count) for index in range(row_count)]
    backward = [(index, (index - 1) % row_count) for index in range(row_count)]
    piece_rows = 4 * width
    chunks = [local[4 * slot : 4 * slot + 4] for slot in range(per_owner)]
    moments = [jnp.zeros((count * width, pairs), jnp.float32) for _ in range(per_owner)]
    grams = [jnp.zeros((piece_rows, piece_rows), jnp.float32) for _ in range(per_owner)]
    held = factor
    held_pieces = []
    rows = jnp.arange(width, dtype=jnp.int32)[None, :]
    pick = (rows == row_lo + jnp.arange(count, dtype=jnp.int32)[:, None]).astype(jnp.bfloat16)
    for step in range(row_count):
        if step + 1 < row_count:
            incoming = [
                lax.ppermute(chunks[slot], "row", forward if slot % 2 == 0 else backward)
                for slot in range(per_owner)
            ]
            held_in = lax.ppermute(held, "row", forward)
        held_pieces.append(held)
        moments, grams = moment_step([pick] * per_owner, chunks, moments, grams)
        if step + 1 < row_count:
            chunks, held = incoming, held_in
    slabs = []
    for slot in range(per_owner):
        moment = moments[slot] / SAMPLES
        gram = grams[slot] / SAMPLES
        slabs.append(cumulant_slab(moment, gram, count, width, row_lo))
    source = (lax.axis_index("row") - jnp.arange(row_count)) % row_count
    stacked = jnp.stack(held_pieces)[source]
    full = jnp.transpose(stacked, (1, 0, 2)).reshape(factor.shape[0], -1)
    for step in range(ITERS):
        grad = jnp.zeros(full.shape, jnp.float32)
        for slot in range(per_owner):
            grad = add_grads(grad, slabs[slot], full, mine[slot], row_lo, count, width)
        grad = all_sum(grad)
        scale = lax.rsqrt(jnp.mean(grad * grad) + 1e-06)
        full = full + step_size * scale * grad
    col_count = factor.shape[1]
    columns = lax.dynamic_slice_in_dim(full, lax.axis_index("row") * col_count, col_count, 1)
    return (jnp.stack(slabs), columns)


def solution(mesh):
    placed = (P("blk", "row"), P(), P(None, "row"))
    return jax.shard_map(
        per_device,
        mesh=mesh,
        in_specs=placed,
        out_specs=(P("blk", "row", None), P(None, "row")),
        check_vma=False,
    )
```
